32 devices in a mesh: seq: 8 (over y, x, core), head: 4 (over z).
Axes of the slice: x: 2, y: 2, z: 4, core: 2. Of those that a mesh axis runs over, the one named last changes fastest.
Arguments:
- x_in: bfloat16 [8, 2048, 2048], P(None, 'seq', 'head'), may hold values from -6 to 6
- b_in: bfloat16 [8, 256, 2048], P(None, 'seq', 'head'), may hold values from -6 to 6
- c_in: bfloat16 [8, 256, 2048], P(None, 'seq', 'head'), may hold values from -6 to 6
- dt_raw: bfloat16 [8, 32, 2048], P(None, 'seq', 'head'), may hold values from -1.4 to 12.9
- cotangent: bfloat16 [8, 2048, 2048], P(None, 'seq', 'head'), may hold values from -6 to 6
- conv_weight: float32 [8, 4, 2560], P('head'), may hold values from -3 to 3
- conv_bias: float32 [8, 2560], P('head'), may hold values from -0.5 to 0.5
- dt_bias: float32 [8, 32], P('head'), may hold values from -7.6 to -3
- a_log: float32 [8, 32], P('head'), may hold values from -3 to 1.39
- d_skip: float32 [8, 32], P('head'), may hold values from 0.5 to 1.5
- doc_lengths: int32 [4], replicated, may hold values from 1 to 896, 2048 in all
Outputs:
- y_out: bfloat16 [8, 2048, 2048], P(None, 'seq', 'head')
- x_grad: bfloat16 [8, 2048, 2048], P(None, 'seq', 'head')
- b_grad: bfloat16 [8, 256, 2048], P(None, 'seq', 'head')
- c_grad: bfloat16 [8, 256, 2048], P(None, 'seq', 'head')
- dt_grad: bfloat16 [8, 32, 2048], P(None, 'seq', 'head')
The draws below stay inside these ranges and needn't reach their ends.
Inputs may be any that keep to these rules, and one draw needn't show every extreme that they name: `doc_lengths`: 4 document lengths that sum to 2048.
All inputs are finite; a program needn't handle non-finite values.
Results may differ from the reference program's by a relative error of at most 0.0025.
Values may be sent and summed in bfloat16 or wider, within the bound.
No kernel may reach another device: no remote copies, remote signals or barrier semaphores. Data moves between devices by JAX's collectives and lax.ppermute only.
A program may use at most 256 MiB of HBM per device.

```python
import math
import jax
import jax.numpy as jnp
import numpy as np
from jax import lax

GROUPS = 8
HEAD_DIM = 64
STATE = 256
TAPS = 4
SPAN = 128
TOK_SHARD = 256
DOCS = 4
GROUP_HEADS = 32
CHANNELS = 2560
PACKED_TOKENS = 2048


reset_count = 3


def head_kind(key):
    picks = jax.random.randint(jax.random.fold_in(key, 11), (GROUPS, GROUP_HEADS), 0, 10)
    limit = 5
    return (picks < limit).astype(jnp.float32)


def draw_a_log(key, part):
    slowly = head_kind(key)
    unit = jax.random.uniform(jax.random.fold_in(key, 12), (GROUPS, GROUP_HEADS), jnp.float32)
    slow_val = jnp.log(0.05) + unit * (jnp.log(0.07) - jnp.log(0.05))
    fast_val = jnp.log(0.5) + unit * (jnp.log(4.0) - jnp.log(0.5))
    return (slowly * slow_val + (1.0 - slowly) * fast_val).astype(jnp.float32)


def draw_dt_bias(key, part):
    slowly = head_kind(key)
    unit = jax.random.uniform(jax.random.fold_in(key, 13), (GROUPS, GROUP_HEADS), jnp.float32)
    slow_val = -7.6 + 0.6 * unit
    fast_val = -4.6 + 1.6 * unit
    return (slowly * slow_val + (1.0 - slowly) * fast_val).astype(jnp.float32)


def draw_dt_raw(key, part):
    rough_key, level_key, sample_key = jax.random.split(key, 3)
    rough = jax.random.uniform(rough_key, (GROUPS, GROUP_HEADS, PACKED_TOKENS), jnp.float32, -0.7, 0.7)
    level = jax.random.uniform(level_key, (GROUPS, GROUP_HEADS, PACKED_TOKENS // TOK_SHARD), jnp.float32, -0.7, 0.7)
    level = jnp.repeat(level, TOK_SHARD, axis=2)
    sample_points = jax.random.randint(sample_key, (reset_count,), 0, PACKED_TOKENS)
    places = jnp.arange(PACKED_TOKENS, dtype=jnp.int32)
    marks = jnp.minimum(jnp.sum((places[:, None] == sample_points[None, :]).astype(jnp.float32), axis=1), 1.0)
    return (rough + level + 11.5 * marks[None, None, :]).astype(jnp.bfloat16)


def shard_levels(rng, shape, cuts, smallest, largest):
    gain, own = 1.0, jax.random.fold_in(rng, 6)
    for position, blocks in cuts:
        heights = jnp.exp(jax.random.uniform(jax.random.fold_in(own, position), (blocks,), jnp.float32, smallest / len(cuts), largest / len(cuts)))
        gain = gain * jnp.repeat(heights, shape[position] // blocks).reshape([-1 if axis == position else 1 for axis in range(len(shape))])
    return gain


def length_profile(amount, total, most, lean):
    portions = [(1 << 20) // math.isqrt(grade ** lean) + 1 for grade in range(2, amount + 1)]
    surplus, holding = total - most - (amount - 1), [1] * (amount - 1)
    while surplus > 0:
        free = [i for i in range(amount - 1) if holding[i] < most]
        pool, budget = sum([portions[i] for i in free]), surplus
        for i in free:
            extra = min(most - holding[i], max(1, budget * portions[i] // pool), surplus)
            holding[i] = holding[i] + extra
            surplus = surplus - extra
    return np.array([most] + holding)


def ragged(rng, count, total, reach, skew):
    if count == 2:
        one = jax.random.randint(rng, (), max(1, total - reach), min(reach, total - 1) + 1)
        return jnp.stack([one, total - one])
    tallies = jnp.asarray(length_profile(count, total, reach, skew), jnp.int32)
    couples = (count - 1) // 2
    source_of, sink = tallies[1:1 + 2 * couples:2], tallies[2:2 + 2 * couples:2]
    room = jnp.minimum(source_of - 1, reach - sink)
    passed = jax.random.randint(jax.random.fold_in(rng, 1), (couples,), 0, 1 << 20) % (room + 1)
    tallies = tallies.at[1:1 + 2 * couples:2].set(source_of - passed).at[2:2 + 2 * couples:2].set(sink + passed)
    return tallies[jax.random.permutation(jax.random.fold_in(rng, 2), count)]


def normal_values(key, extent, scale, most, shards=(), held_as=jnp.bfloat16):
    gain = shard_levels(key, extent, shards, -0.22, 0.18) if shards else 1.0
    drawn = jax.random.normal(key, extent, jnp.float32) * scale * gain
    return jnp.minimum(jnp.maximum(drawn, -most), most).astype(held_as)


def setup_inputs(seed: int = 0) -> dict:
    key_of = jax.random.split(jax.random.key(seed), 12)
    return {
        "x_in": normal_values(key_of[0], (GROUPS, GROUP_HEADS * HEAD_DIM, PACKED_TOKENS), 1.0, 6.0, ((1, 8), (2, 4))),
        "b_in": normal_values(key_of[1], (GROUPS, STATE, PACKED_TOKENS), 1.0, 6.0, ((1, 8), (2, 4))),
        "c_in": normal_values(key_of[2], (GROUPS, STATE, PACKED_TOKENS), 1.0, 6.0, ((1, 8), (2, 4))),
        "dt_raw": draw_dt_raw(jax.random.fold_in(key_of[11], 71), 0),
        "cotangent": normal_values(key_of[4], (GROUPS, GROUP_HEADS * HEAD_DIM, PACKED_TOKENS), 1.0, 6.0, ((1, 8), (2, 4))),
        "conv_weight": normal_values(key_of[5], (GROUPS, TAPS, CHANNELS), TAPS ** -0.5, 3.0, ((0, 4),), jnp.float32),
        "conv_bias": jnp.clip(jax.random.uniform(key_of[6], (GROUPS, CHANNELS), jnp.float32, -0.5, 0.5) * shard_levels(key_of[6], (GROUPS, CHANNELS), ((0, 4),), -0.4, 0.0), -0.5, 0.5),
        "dt_bias": draw_dt_bias(jax.random.fold_in(key_of[11], 71), 0),
        "a_log": draw_a_log(jax.random.fold_in(key_of[11], 71), 0),
        "d_skip": jnp.clip(0.5 + 1.0 * jax.random.uniform(key_of[9], (GROUPS, GROUP_HEADS), jnp.float32) ** shard_levels(key_of[9], (GROUPS, GROUP_HEADS), ((0, 4),), -0.2, 0.2), 0.5, 1.5),
        "doc_lengths": ragged(key_of[10], DOCS, PACKED_TOKENS, PACKED_TOKENS // 2 - TOK_SHARD // 2, 1).astype(jnp.int32),
    }


precise = lax.Precision.HIGHEST

def segment_ids(positions, doc_lengths):
    ends = jnp.cumsum(doc_lengths).astype(jnp.int32)
    counted = lax.optimization_barrier(jnp.sum((ends[None, :] <= positions[:, None]).astype(jnp.int32), axis=1)).astype(jnp.int32)
    return jnp.where(positions >= 0, counted, -1).astype(jnp.int32)

def conv_silu(padded, weight, bias, segment_extended, length):
    total = jnp.zeros((padded.shape[0], length), jnp.float32) + bias[:, None]
    for offset in range(TAPS):
        same_doc = (segment_extended[offset:offset + length] == segment_extended[TAPS - 1:]).astype(jnp.float32)
        total = total + weight[offset][:, None] * padded[:, offset:offset + length] * same_doc[None, :]
    return jax.nn.silu(total)

def span_terms(x_conv, b_conv, c_conv, step_size, log_decay, seg_tok, seg_before, skip_gain):
    n_heads, length = step_size.shape
    blocks = length // SPAN
    x_four = x_conv.reshape(n_heads, HEAD_DIM, blocks, SPAN)
    b_three = b_conv.reshape(STATE, blocks, SPAN)
    c_three = c_conv.reshape(STATE, blocks, SPAN)
    step_three = step_size.reshape(n_heads, blocks, SPAN)
    seg_two = seg_tok.reshape(blocks, SPAN)
    rows_idx = lax.broadcasted_iota(jnp.int32, (SPAN, SPAN), 0)
    cols_idx = lax.broadcasted_iota(jnp.int32, (SPAN, SPAN), 1)
    lower = (rows_idx >= cols_idx).astype(jnp.float32)
    cumul = jnp.einsum('hcj,ij->hci', log_decay.reshape(n_heads, blocks, SPAN), lower, precision=precise)
    mask_doc = lower[None] * (seg_two[:, :, None] == seg_two[:, None, :]).astype(jnp.float32)
    decay = jnp.exp(jnp.minimum(cumul[:, :, :, None] - cumul[:, :, None, :], 0.0)) * mask_doc[None]
    scores = jnp.einsum('nci,ncj->cij', c_three, b_three, precision=precise)
    weighted = x_four * step_three[:, None]
    y_intra = jnp.einsum('hcij,hpcj->hpci', decay * scores[None], weighted, precision=precise)
    y_intra = y_intra + skip_gain[:, None, None, None] * x_four
    last_cum = cumul[:, :, -1:]
    keep_end = jnp.exp(last_cum - cumul) * (seg_two == seg_two[:, -1:]).astype(jnp.float32)[None]
    states = jnp.einsum('hpcj,hcj,ncj->hcpn', weighted, keep_end, b_three, precision=precise)
    prev_seg = jnp.concatenate([seg_before[None], seg_two[:-1, -1]]).astype(jnp.int32)
    entry = jnp.exp(cumul) * (seg_two == prev_seg[:, None]).astype(jnp.float32)[None]
    carry = jnp.exp(last_cum[:, :, 0]) * (seg_two[:, -1] == prev_seg).astype(jnp.float32)[None]
    return (y_intra, c_three, entry, carry, states)

def group_terms(raw_chan, rim_chan, dt_pre, weight, bias, bias_dt, log_rate, skip_gain, segment_extended):
    n_heads = dt_pre.shape[0]
    length = raw_chan.shape[1]
    padded = jnp.concatenate([rim_chan, raw_chan], axis=1)
    active = conv_silu(padded, weight, bias, segment_extended, length)
    split_at = n_heads * HEAD_DIM
    x_conv = active[:split_at]
    b_conv = active[split_at:split_at + STATE]
    c_conv = active[split_at + STATE:]
    step_size = jax.nn.softplus(dt_pre + bias_dt[:, None])
    log_decay = step_size * (-jnp.exp(log_rate))[:, None]
    return span_terms(x_conv, b_conv, c_conv, step_size, log_decay, segment_extended[TAPS - 1:], segment_extended[TAPS - 2], skip_gain)

def span_fold(carry, states, state_start):

    def advance(running, pieces):
        factor, piece = pieces
        return (factor[:, None, None] * running + piece, running)
    state_end, starts = lax.scan(advance, state_start, (carry.T, jnp.moveaxis(states, 1, 0)))
    return (starts, state_end)

def assemble(y_intra, c_three, entry, carry, states, state_start):
    starts, state_end = span_fold(carry, states, state_start)
    y_full = y_intra + jnp.einsum('nci,hci,chpn->hpci', c_three, entry, starts, precision=precise)
    return (y_full.reshape(y_full.shape[0] * y_full.shape[1], -1), state_end)

def reference(x_in, b_in, c_in, dt_raw, cotangent, conv_weight, conv_bias, dt_bias, a_log, d_skip, doc_lengths):
    positions = jnp.arange(-(TAPS - 1), PACKED_TOKENS, dtype=jnp.int32)
    segment_extended = segment_ids(positions, doc_lengths)

    def one_group(items):
        x_grp, b_grp, c_grp, dt_grp, cot_grp, w_grp, cb_grp, db_grp, al_grp, ds_grp = items
        n_heads = dt_grp.shape[0]

        def forward(x_float, b_float, c_float, dt_float):
            raw_chan = jnp.concatenate([x_float, b_float, c_float], axis=0)
            rim_chan = jnp.zeros((raw_chan.shape[0], TAPS - 1), jnp.float32)
            terms = group_terms(raw_chan, rim_chan, dt_float, w_grp, cb_grp, db_grp, al_grp, ds_grp, segment_extended)
            state_start = jnp.zeros((n_heads, HEAD_DIM, STATE), jnp.float32)
            return assemble(*terms, state_start)[0]
        y_full, pull = jax.vjp(forward, x_grp.astype(jnp.float32), b_grp.astype(jnp.float32), c_grp.astype(jnp.float32), dt_grp.astype(jnp.float32))
        gx_full, gb_full, gc_full, gd_full = pull(cot_grp.astype(jnp.float32))
        return (y_full.astype(jnp.bfloat16), gx_full.astype(jnp.bfloat16), gb_full.astype(jnp.bfloat16), gc_full.astype(jnp.bfloat16), gd_full.astype(jnp.bfloat16))
    y_out, x_grad, b_grad, c_grad, dt_grad = lax.map(one_group, (x_in, b_in, c_in, dt_raw, cotangent, conv_weight, conv_bias, dt_bias, a_log, d_skip))
    return (y_out, x_grad, b_grad, c_grad, dt_grad)
```

```python
import jax
import jax.numpy as jnp
from jax import lax
from jax.sharding import PartitionSpec as P

HEAD_DIM = 64
STATE = 256
TAPS = 4
SPAN = 128


precise = lax.Precision.HIGHEST


def passed_along(value, axis, steps):
    count = lax.axis_size(axis)
    first, last = (max(0, -steps), min(count, count - steps))
    return lax.ppermute(value, axis, [(source, source + steps) for source in range(first, last)])


def carried_in(array, axis, combine, identity, reverse):
    peers, index = (lax.axis_size(axis), lax.axis_index(axis))
    everything = jax.tree.map(lambda part: lax.all_gather(part, axis), array)
    start = jax.tree.map(
        lambda part, zero: jnp.broadcast_to(jnp.asarray(zero, part.dtype), part.shape),
        array,
        identity,
    )

    def lap(k, before):
        at = peers - 1 - k if reverse else k
        reached = at > index if reverse else at < index
        new = combine(before, jax.tree.map(lambda part: part[at], everything))
        return jax.tree.map(lambda a, b: jnp.where(reached, a, b), new, before)

    return lax.fori_loop(0, peers, lap, start)


def segment_ids(positions, doc_lengths):
    ends = jnp.cumsum(doc_lengths)
    counted = jnp.sum((ends[None, :] <= positions[:, None]).astype(jnp.int32), axis=1)
    return jnp.where(positions >= 0, counted, -1)


def conv_silu(padded, weight, bias, segment_extended, length):
    total = jnp.zeros((padded.shape[0], length), jnp.float32) + bias[:, None]
    for offset in range(TAPS):
        same_doc = (
            segment_extended[offset : offset + length] == segment_extended[TAPS - 1 :]
        ).astype(jnp.float32)
        total = (
            total
            + weight[offset][:, None] * padded[:, offset : offset + length] * same_doc[None, :]
        )
    return jax.nn.silu(total)


def span_terms(x_conv, b_conv, c_conv, step_size, log_decay, seg_tok, seg_before, skip_gain):
    n_heads, length = step_size.shape
    blocks = length // SPAN
    x_four = x_conv.reshape(n_heads, HEAD_DIM, blocks, SPAN)
    b_three = b_conv.reshape(STATE, blocks, SPAN)
    c_three = c_conv.reshape(STATE, blocks, SPAN)
    step_three = step_size.reshape(n_heads, blocks, SPAN)
    seg_two = seg_tok.reshape(blocks, SPAN)
    rows_idx = lax.broadcasted_iota(jnp.int32, (SPAN, SPAN), 0)
    cols_idx = lax.broadcasted_iota(jnp.int32, (SPAN, SPAN), 1)
    lower = (rows_idx >= cols_idx).astype(jnp.float32)
    cumul = jnp.einsum(
        "hcj,ij->hci", log_decay.reshape(n_heads, blocks, SPAN), lower, precision=precise
    )
    mask_doc = lower[None] * (seg_two[:, :, None] == seg_two[:, None, :]).astype(jnp.float32)
    decay = jnp.exp(jnp.minimum(cumul[:, :, :, None] - cumul[:, :, None, :], 0.0)) * mask_doc[None]
    scores = jnp.einsum("nci,ncj->cij", c_three, b_three, precision=precise)
    weighted = x_four * step_three[:, None]
    y_intra = jnp.einsum("hcij,hpcj->hpci", decay * scores[None], weighted, precision=precise)
    y_intra = y_intra + skip_gain[:, None, None, None] * x_four
    last_cum = cumul[:, :, -1:]
    keep_end = jnp.exp(last_cum - cumul) * (seg_two == seg_two[:, -1:]).astype(jnp.float32)[None]
    states = jnp.einsum("hpcj,hcj,ncj->hcpn", weighted, keep_end, b_three, precision=precise)
    prev_seg = jnp.concatenate([seg_before[None], seg_two[:-1, -1]])
    entry = jnp.exp(cumul) * (seg_two == prev_seg[:, None]).astype(jnp.float32)[None]
    carry = jnp.exp(last_cum[:, :, 0]) * (seg_two[:, -1] == prev_seg).astype(jnp.float32)[None]
    return (y_intra, c_three, entry, carry, states)


def group_terms(
    raw_chan, rim_chan, dt_pre, weight, bias, bias_dt, log_rate, skip_gain, segment_extended
):
    n_heads = dt_pre.shape[0]
    length = raw_chan.shape[1]
    padded = jnp.concatenate([rim_chan, raw_chan], axis=1)
    active = conv_silu(padded, weight, bias, segment_extended, length)
    split_at = n_heads * HEAD_DIM
    x_conv = active[:split_at]
    b_conv = active[split_at : split_at + STATE]
    c_conv = active[split_at + STATE :]
    step_size = jax.nn.softplus(dt_pre + bias_dt[:, None])
    log_decay = step_size * (-jnp.exp(log_rate))[:, None]
    return span_terms(
        x_conv,
        b_conv,
        c_conv,
        step_size,
        log_decay,
        segment_extended[TAPS - 1 :],
        segment_extended[TAPS - 2],
        skip_gain,
    )


def span_fold(carry, states, state_start):

    def span_advance(running, pieces):
        factor, piece = pieces
        return (factor[:, None, None] * running + piece, running)

    state_end, starts = lax.scan(span_advance, state_start, (carry.T, jnp.moveaxis(states, 1, 0)))
    return (starts, state_end)


def assemble(y_intra, c_three, entry, carry, states, state_start):
    starts, state_end = span_fold(carry, states, state_start)
    y_full = y_intra + jnp.einsum("nci,hci,chpn->hpci", c_three, entry, starts, precision=precise)
    return (y_full.reshape(y_full.shape[0] * y_full.shape[1], -1), state_end)


def reach(carry):

    def reach_advance(product, factor):
        return (product * factor, product)

    total, before = lax.scan(
        reach_advance, jnp.ones(carry.shape[:-1], jnp.float32), jnp.moveaxis(carry, -1, 0)
    )
    return (jnp.moveaxis(before, 0, -1), total)


def compose_fwd(preceding_states, later):
    return (
        preceding_states[0] * later[0],
        later[0][..., None, None] * preceding_states[1] + later[1],
    )


def compose_back(preceding_states, later):
    return (
        later[0] * preceding_states[0],
        later[1] + later[0][..., None, None] * preceding_states[1],
    )


def shards(
    x_in, b_in, c_in, dt_raw, cotangent, conv_weight, conv_bias, dt_bias, a_log, d_skip, doc_lengths
):
    lane = lax.axis_index("seq")
    x_width = x_in.shape[1]
    n_heads = dt_raw.shape[1]
    length = x_in.shape[2]
    blocks = length // SPAN
    b_full = lax.all_gather(b_in, "seq", axis=1, tiled=True)
    c_full = lax.all_gather(c_in, "seq", axis=1, tiled=True)
    weight_all = lax.all_gather(conv_weight, "head", axis=0, tiled=True)
    bias_all = lax.all_gather(conv_bias, "head", axis=0, tiled=True)
    dt_bias_all = lax.all_gather(dt_bias, "head", axis=0, tiled=True)
    a_log_all = lax.all_gather(a_log, "head", axis=0, tiled=True)
    d_skip_all = lax.all_gather(d_skip, "head", axis=0, tiled=True)
    x_total = weight_all.shape[2] - 2 * STATE

    def own_channels(table):
        mine = lax.dynamic_slice_in_dim(table, lane * x_width, x_width, axis=table.ndim - 1)
        return jnp.concatenate([mine, table[..., x_total:]], axis=table.ndim - 1)

    weight_here = own_channels(weight_all)
    bias_here = own_channels(bias_all)
    dt_bias_here = lax.dynamic_slice_in_dim(dt_bias_all, lane * n_heads, n_heads, axis=1)
    a_log_here = lax.dynamic_slice_in_dim(a_log_all, lane * n_heads, n_heads, axis=1)
    d_skip_here = lax.dynamic_slice_in_dim(d_skip_all, lane * n_heads, n_heads, axis=1)
    groups_here = x_in.shape[0]
    raw_chan = jnp.concatenate([x_in, b_full, c_full], axis=1)
    rim_chan = passed_along(raw_chan[:, :, length - (TAPS - 1) :], "head", 1)
    rank = lax.axis_index("head")
    positions = rank * length + jnp.arange(-(TAPS - 1), length, dtype=jnp.int32)
    segment_extended = segment_ids(positions, doc_lengths)

    def local_terms(raw_float, rim_float, dt_float):
        return jax.vmap(group_terms, in_axes=(0, 0, 0, 0, 0, 0, 0, 0, None))(
            raw_float,
            rim_float,
            dt_float,
            weight_here,
            bias_here,
            dt_bias_here,
            a_log_here,
            d_skip_here,
            segment_extended,
        )

    terms, pull_terms = jax.vjp(
        local_terms,
        raw_chan.astype(jnp.float32),
        rim_chan.astype(jnp.float32),
        dt_raw.astype(jnp.float32),
    )
    y_intra, c_three, entry, carry, states = terms
    before, total = reach(carry)
    state_zero = jnp.zeros((groups_here, n_heads, HEAD_DIM, STATE), jnp.float32)
    _, summary = jax.vmap(span_fold)(carry, states, state_zero)
    identity = (jnp.ones_like(total), jnp.zeros_like(summary))
    state_in = carried_in((total, summary), "head", compose_fwd, identity, False)[1]

    def finish(pieces, state_start):
        return jax.vmap(assemble)(
            pieces[0], pieces[1], pieces[2], pieces[3], pieces[4], state_start
        )

    (y_scan, state_out), pull_out = jax.vjp(finish, terms, state_in)
    y_out = y_scan.astype(jnp.bfloat16)
    cot_float = cotangent.astype(jnp.float32)
    cot_five = cot_float.reshape(groups_here, n_heads, HEAD_DIM, blocks, SPAN)
    local_grad = jnp.einsum(
        "ghpci,ghci,gnci->ghpn", cot_five, entry * before[..., None], c_three, precision=precise
    )
    grad_out = carried_in((total, local_grad), "head", compose_back, identity, True)[1]
    d_terms, _ = pull_out((cot_float, grad_out))
    d_raw, d_rim, d_dt = pull_terms(d_terms)
    returned = passed_along(d_rim, "head", -1)
    cut_at = length - (TAPS - 1)
    d_raw = jnp.concatenate([d_raw[:, :, :cut_at], d_raw[:, :, cut_at:] + returned], axis=2)
    x_grad = d_raw[:, :x_width].astype(jnp.bfloat16)
    b_grad = lax.psum_scatter(
        d_raw[:, x_width : x_width + STATE], "seq", scatter_dimension=1, tiled=True
    ).astype(jnp.bfloat16)
    c_grad = lax.psum_scatter(
        d_raw[:, x_width + STATE :], "seq", scatter_dimension=1, tiled=True
    ).astype(jnp.bfloat16)
    dt_grad = d_dt.astype(jnp.bfloat16)
    return (y_out, x_grad, b_grad, c_grad, dt_grad)


def solution(mesh):
    return jax.shard_map(
        shards,
        mesh=mesh,
        in_specs=(
            P(None, "seq", "head"),
            P(None, "seq", "head"),
            P(None, "seq", "head"),
            P(None, "seq", "head"),
            P(None, "seq", "head"),
            P("head", None, None),
            P("head", None),
            P("head", None),
            P("head", None),
            P("head", None),
            P(),
        ),
        out_specs=(
            P(None, "seq", "head"),
            P(None, "seq", "head"),
            P(None, "seq", "head"),
            P(None, "seq", "head"),
            P(None, "seq", "head"),
        ),
        check_vma=False,
    )
```

```python
import jax
import jax.numpy as jnp
from jax import lax
from jax.sharding import PartitionSpec as P

HEAD_DIM = 64
STATE = 256
TAPS = 4
SPAN = 128


precise = lax.Precision.HIGHEST


def passed_along(value, axis, steps):
    count = lax.axis_size(axis)
    first, last = (max(0, -steps), min(count, count - steps))
    return lax.ppermute(value, axis, [(source, source + steps) for source in range(first, last)])


def carried_in(totals, pieces, axis, reverse):
    peers, index = (lax.axis_size(axis), lax.axis_index(axis))
    every_total = lax.all_gather(totals, axis)
    every_piece = lax.all_gather(pieces, axis)
    idx = jnp.arange(peers)
    if reverse:
        between = (index < idx[None, :]) & (idx[None, :] < idx[:, None])
        valid = idx > index
    else:
        between = (idx[:, None] < idx[None, :]) & (idx[None, :] < index)
        valid = idx < index
    picked = jnp.where(between[:, :, None, None], every_total[None], 1.0)
    weight = jnp.prod(picked, axis=1) * valid.astype(jnp.float32)[:, None, None]
    return jnp.sum(weight[..., None, None] * every_piece, axis=0)


def segment_ids(positions, doc_lengths):
    ends = jnp.cumsum(doc_lengths)
    counted = jnp.sum((ends[None, :] <= positions[:, None]).astype(jnp.int32), axis=1)
    return jnp.where(positions >= 0, counted, -1)


def conv_silu(padded, weight, bias, segment_extended, length):
    total = jnp.zeros((padded.shape[0], length), jnp.float32) + bias[:, None]
    for offset in range(TAPS):
        same_doc = (
            segment_extended[offset : offset + length] == segment_extended[TAPS - 1 :]
        ).astype(jnp.float32)
        total = (
            total
            + weight[offset][:, None] * padded[:, offset : offset + length] * same_doc[None, :]
        )
    return jax.nn.silu(total)


def span_terms(x_conv, b_conv, c_conv, step_size, log_decay, seg_tok, seg_before, skip_gain):
    n_heads, length = step_size.shape
    blocks = length // SPAN
    x_four = x_conv.reshape(n_heads, HEAD_DIM, blocks, SPAN)
    b_three = b_conv.reshape(STATE, blocks, SPAN)
    c_three = c_conv.reshape(STATE, blocks, SPAN)
    step_three = step_size.reshape(n_heads, blocks, SPAN)
    seg_two = seg_tok.reshape(blocks, SPAN)
    rows_idx = lax.broadcasted_iota(jnp.int32, (SPAN, SPAN), 0)
    cols_idx = lax.broadcasted_iota(jnp.int32, (SPAN, SPAN), 1)
    lower = (rows_idx >= cols_idx).astype(jnp.float32)
    cumul = jnp.einsum(
        "hcj,ij->hci", log_decay.reshape(n_heads, blocks, SPAN), lower, precision=precise
    )
    mask_doc = lower[None] * (seg_two[:, :, None] == seg_two[:, None, :]).astype(jnp.float32)
    decay = jnp.exp(jnp.minimum(cumul[:, :, :, None] - cumul[:, :, None, :], 0.0)) * mask_doc[None]
    scores = jnp.einsum("nci,ncj->cij", c_three, b_three, precision=precise)
    weighted = x_four * step_three[:, None]
    y_intra = jnp.einsum("hcij,hpcj->hpci", decay * scores[None], weighted, precision=precise)
    y_intra = y_intra + skip_gain[:, None, None, None] * x_four
    last_cum = cumul[:, :, -1:]
    keep_end = jnp.exp(last_cum - cumul) * (seg_two == seg_two[:, -1:]).astype(jnp.float32)[None]
    states = jnp.einsum("hpcj,hcj,ncj->hcpn", weighted, keep_end, b_three, precision=precise)
    prev_seg = jnp.concatenate([seg_before[None], seg_two[:-1, -1]])
    entry = jnp.exp(cumul) * (seg_two == prev_seg[:, None]).astype(jnp.float32)[None]
    carry = jnp.exp(last_cum[:, :, 0]) * (seg_two[:, -1] == prev_seg).astype(jnp.float32)[None]
    return (y_intra, c_three, entry, carry, states)


def group_terms(
    raw_chan, rim_chan, dt_pre, weight, bias, bias_dt, log_rate, skip_gain, segment_extended
):
    n_heads = dt_pre.shape[0]
    length = raw_chan.shape[1]
    padded = jnp.concatenate([rim_chan, raw_chan], axis=1)
    active = conv_silu(padded, weight, bias, segment_extended, length)
    split_at = n_heads * HEAD_DIM
    x_conv = active[:split_at]
    b_conv = active[split_at : split_at + STATE]
    c_conv = active[split_at + STATE :]
    step_size = jax.nn.softplus(dt_pre + bias_dt[:, None])
    log_decay = step_size * (-jnp.exp(log_rate))[:, None]
    return span_terms(
        x_conv,
        b_conv,
        c_conv,
        step_size,
        log_decay,
        segment_extended[TAPS - 1 :],
        segment_extended[TAPS - 2],
        skip_gain,
    )


def weighted_sum(weight, stacked):
    return jnp.sum(weight[..., None, None] * stacked, axis=-3)


def span_fold(carry, states, state_start):
    blocks = carry.shape[-1]
    idx = jnp.arange(blocks)
    inside = (idx[None, :, None] < idx[None, None, :]) & (idx[None, None, :] < idx[:, None, None])
    link = jnp.prod(jnp.where(inside[None], carry[:, None, None, :], 1.0), axis=-1)
    link = link * (idx[None, :] < idx[:, None]).astype(jnp.float32)[None]
    lead = jnp.prod(jnp.where((idx[None, :] < idx[:, None])[None], carry[:, None, :], 1.0), axis=-1)
    tail = jnp.prod(jnp.where((idx[None, :] > idx[:, None])[None], carry[:, None, :], 1.0), axis=-1)
    starts = weighted_sum(link, states[:, None]) + lead[..., None, None] * state_start[:, None]
    state_end = weighted_sum(tail, states) + jnp.prod(carry, axis=-1)[:, None, None] * state_start
    return (jnp.moveaxis(starts, 1, 0), state_end)


def assemble(y_intra, c_three, entry, carry, states, state_start):
    starts, state_end = span_fold(carry, states, state_start)
    y_full = y_intra + jnp.einsum("nci,hci,chpn->hpci", c_three, entry, starts, precision=precise)
    return (y_full.reshape(y_full.shape[0] * y_full.shape[1], -1), state_end)


def reach(carry):

    def reach_advance(product, factor):
        return (product * factor, product)

    total, before = lax.scan(
        reach_advance, jnp.ones(carry.shape[:-1], jnp.float32), jnp.moveaxis(carry, -1, 0)
    )
    return (jnp.moveaxis(before, 0, -1), total)


def shards(
    x_in, b_in, c_in, dt_raw, cotangent, conv_weight, conv_bias, dt_bias, a_log, d_skip, doc_lengths
):
    lane = lax.axis_index("seq")
    x_width = x_in.shape[1]
    n_heads = dt_raw.shape[1]
    length = x_in.shape[2]
    blocks = length // SPAN
    b_full = lax.all_gather(b_in, "seq", axis=1, tiled=True)
    c_full = lax.all_gather(c_in, "seq", axis=1, tiled=True)
    groups_held = conv_weight.shape[0]
    packed = jnp.concatenate(
        [
            conv_weight.reshape(groups_held, -1),
            conv_bias,
            dt_bias,
            a_log,
            d_skip,
        ],
        axis=1,
    )
    packed_all = lax.all_gather(packed, "head", axis=0, tiled=True)
    cuts = [conv_weight[0].size, conv_bias.shape[1], dt_bias.shape[1], a_log.shape[1]]
    bounds = [sum(cuts[:k]) for k in range(len(cuts) + 1)]
    weight_all = packed_all[:, : bounds[1]].reshape((-1,) + conv_weight.shape[1:])
    bias_all = packed_all[:, bounds[1] : bounds[2]]
    dt_bias_all = packed_all[:, bounds[2] : bounds[3]]
    a_log_all = packed_all[:, bounds[3] : bounds[4]]
    d_skip_all = packed_all[:, bounds[4] :]
    x_total = weight_all.shape[2] - 2 * STATE

    def own_channels(table):
        mine = lax.dynamic_slice_in_dim(table, lane * x_width, x_width, axis=table.ndim - 1)
        return jnp.concatenate([mine, table[..., x_total:]], axis=table.ndim - 1)

    weight_here = own_channels(weight_all)
    bias_here = own_channels(bias_all)
    dt_bias_here = lax.dynamic_slice_in_dim(dt_bias_all, lane * n_heads, n_heads, axis=1)
    a_log_here = lax.dynamic_slice_in_dim(a_log_all, lane * n_heads, n_heads, axis=1)
    d_skip_here = lax.dynamic_slice_in_dim(d_skip_all, lane * n_heads, n_heads, axis=1)
    groups_here = x_in.shape[0]
    raw_chan = jnp.concatenate([x_in, b_full, c_full], axis=1)
    rim_chan = passed_along(raw_chan[:, :, length - (TAPS - 1) :], "head", 1)
    rank = lax.axis_index("head")
    positions = rank * length + jnp.arange(-(TAPS - 1), length, dtype=jnp.int32)
    segment_extended = segment_ids(positions, doc_lengths)

    def local_terms(raw_float, rim_float, dt_float):
        return jax.vmap(group_terms, in_axes=(0, 0, 0, 0, 0, 0, 0, 0, None))(
            raw_float,
            rim_float,
            dt_float,
            weight_here,
            bias_here,
            dt_bias_here,
            a_log_here,
            d_skip_here,
            segment_extended,
        )

    terms, pull_terms = jax.vjp(
        local_terms,
        raw_chan.astype(jnp.float32),
        rim_chan.astype(jnp.float32),
        dt_raw.astype(jnp.float32),
    )
    y_intra, c_three, entry, carry, states = terms
    before, total = reach(carry)
    state_zero = jnp.zeros((groups_here, n_heads, HEAD_DIM, STATE), jnp.float32)
    _, summary = jax.vmap(span_fold)(carry, states, state_zero)
    state_in = carried_in(total, summary, "head", False)

    def finish(pieces, state_start):
        return jax.vmap(assemble)(
            pieces[0], pieces[1], pieces[2], pieces[3], pieces[4], state_start
        )

    (y_scan, state_out), pull_out = jax.vjp(finish, terms, state_in)
    y_out = y_scan.astype(jnp.bfloat16)
    cot_float = cotangent.astype(jnp.float32)
    cot_five = cot_float.reshape(groups_here, n_heads, HEAD_DIM, blocks, SPAN)
    local_grad = jnp.einsum(
        "ghpci,ghci,gnci->ghpn", cot_five, entry * before[..., None], c_three, precision=precise
    )
    grad_out = carried_in(total, local_grad, "head", True)
    d_terms, _ = pull_out((cot_float, grad_out))
    d_raw, d_rim, d_dt = pull_terms(d_terms)
    returned = passed_along(d_rim, "head", -1)
    cut_at = length - (TAPS - 1)
    d_raw = jnp.concatenate([d_raw[:, :, :cut_at], d_raw[:, :, cut_at:] + returned], axis=2)
    x_grad = d_raw[:, :x_width].astype(jnp.bfloat16)
    b_grad = lax.psum_scatter(
        d_raw[:, x_width : x_width + STATE], "seq", scatter_dimension=1, tiled=True
    ).astype(jnp.bfloat16)
    c_grad = lax.psum_scatter(
        d_raw[:, x_width + STATE :], "seq", scatter_dimension=1, tiled=True
    ).astype(jnp.bfloat16)
    dt_grad = d_dt.astype(jnp.bfloat16)
    return (y_out, x_grad, b_grad, c_grad, dt_grad)


def solution(mesh):
    return jax.shard_map(
        shards,
        mesh=mesh,
        in_specs=(
            P(None, "seq", "head"),
            P(None, "seq", "head"),
            P(None, "seq", "head"),
            P(None, "seq", "head"),
            P(None, "seq", "head"),
            P("head", None, None),
            P("head", None),
            P("head", None),
            P("head", None),
            P("head", None),
            P(),
        ),
        out_specs=(
            P(None, "seq", "head"),
            P(None, "seq", "head"),
            P(None, "seq", "head"),
            P(None, "seq", "head"),
            P(None, "seq", "head"),
        ),
        check_vma=False,
    )
```

```python
import jax
import jax.numpy as jnp
from jax import lax
from jax.sharding import PartitionSpec as P

HEAD_DIM = 64
STATE = 256
TAPS = 4
SPAN = 128


precise = lax.Precision.HIGHEST


def passed_along(value, axis, steps):
    count = lax.axis_size(axis)
    first, last = (max(0, -steps), min(count, count - steps))
    return lax.ppermute(value, axis, [(source, source + steps) for source in range(first, last)])


def carried_in(totals, pieces, axis, reverse):
    steps = -1 if reverse else 1
    factor = totals[..., None, None]
    received = passed_along(pieces, axis, steps)
    for _ in range(lax.axis_size(axis) - 2):
        received = passed_along(factor * received + pieces, axis, steps)
    return received


def segment_ids(positions, doc_lengths):
    ends = jnp.cumsum(doc_lengths)
    counted = jnp.sum((ends[None, :] <= positions[:, None]).astype(jnp.int32), axis=1)
    return jnp.where(positions >= 0, counted, -1)


def conv_silu(padded, weight, bias, segment_extended, length):
    total = jnp.zeros((padded.shape[0], length), jnp.float32) + bias[:, None]
    for offset in range(TAPS):
        same_doc = (
            segment_extended[offset : offset + length] == segment_extended[TAPS - 1 :]
        ).astype(jnp.float32)
        total = (
            total
            + weight[offset][:, None] * padded[:, offset : offset + length] * same_doc[None, :]
        )
    return jax.nn.silu(total)


def span_terms(x_conv, b_conv, c_conv, step_size, log_decay, seg_tok, seg_before, skip_gain):
    n_heads, length = step_size.shape
    blocks = length // SPAN
    x_four = x_conv.reshape(n_heads, HEAD_DIM, blocks, SPAN)
    b_three = b_conv.reshape(STATE, blocks, SPAN)
    c_three = c_conv.reshape(STATE, blocks, SPAN)
    step_three = step_size.reshape(n_heads, blocks, SPAN)
    seg_two = seg_tok.reshape(blocks, SPAN)
    rows_idx = lax.broadcasted_iota(jnp.int32, (SPAN, SPAN), 0)
    cols_idx = lax.broadcasted_iota(jnp.int32, (SPAN, SPAN), 1)
    lower = (rows_idx >= cols_idx).astype(jnp.float32)
    cumul = jnp.einsum(
        "hcj,ij->hci", log_decay.reshape(n_heads, blocks, SPAN), lower, precision=precise
    )
    mask_doc = lower[None] * (seg_two[:, :, None] == seg_two[:, None, :]).astype(jnp.float32)
    decay = jnp.exp(jnp.minimum(cumul[:, :, :, None] - cumul[:, :, None, :], 0.0)) * mask_doc[None]
    scores = jnp.einsum("nci,ncj->cij", c_three, b_three, precision=precise)
    weighted = x_four * step_three[:, None]
    y_intra = jnp.einsum("hcij,hpcj->hpci", decay * scores[None], weighted, precision=precise)
    y_intra = y_intra + skip_gain[:, None, None, None] * x_four
    last_cum = cumul[:, :, -1:]
    keep_end = jnp.exp(last_cum - cumul) * (seg_two == seg_two[:, -1:]).astype(jnp.float32)[None]
    states = jnp.einsum("hpcj,hcj,ncj->hcpn", weighted, keep_end, b_three, precision=precise)
    prev_seg = jnp.concatenate([seg_before[None], seg_two[:-1, -1]])
    entry = jnp.exp(cumul) * (seg_two == prev_seg[:, None]).astype(jnp.float32)[None]
    carry = jnp.exp(last_cum[:, :, 0]) * (seg_two[:, -1] == prev_seg).astype(jnp.float32)[None]
    return (y_intra, c_three, entry, carry, states)


def group_terms(
    raw_chan, rim_chan, dt_pre, weight, bias, bias_dt, log_rate, skip_gain, segment_extended
):
    n_heads = dt_pre.shape[0]
    length = raw_chan.shape[1]
    padded = jnp.concatenate([rim_chan, raw_chan], axis=1)
    active = conv_silu(padded, weight, bias, segment_extended, length)
    split_at = n_heads * HEAD_DIM
    x_conv = active[:split_at]
    b_conv = active[split_at : split_at + STATE]
    c_conv = active[split_at + STATE :]
    step_size = jax.nn.softplus(dt_pre + bias_dt[:, None])
    log_decay = step_size * (-jnp.exp(log_rate))[:, None]
    return span_terms(
        x_conv,
        b_conv,
        c_conv,
        step_size,
        log_decay,
        segment_extended[TAPS - 1 :],
        segment_extended[TAPS - 2],
        skip_gain,
    )


def weighted_sum(weight, stacked):
    return jnp.sum(weight[..., None, None] * stacked, axis=-3)


def span_fold(carry, states, state_start):
    blocks = carry.shape[-1]
    idx = jnp.arange(blocks)
    inside = (idx[None, :, None] < idx[None, None, :]) & (idx[None, None, :] < idx[:, None, None])
    link = jnp.prod(jnp.where(inside[None], carry[:, None, None, :], 1.0), axis=-1)
    link = link * (idx[None, :] < idx[:, None]).astype(jnp.float32)[None]
    lead = jnp.prod(jnp.where((idx[None, :] < idx[:, None])[None], carry[:, None, :], 1.0), axis=-1)
    tail = jnp.prod(jnp.where((idx[None, :] > idx[:, None])[None], carry[:, None, :], 1.0), axis=-1)
    starts = weighted_sum(link, states[:, None]) + lead[..., None, None] * state_start[:, None]
    state_end = weighted_sum(tail, states) + jnp.prod(carry, axis=-1)[:, None, None] * state_start
    return (jnp.moveaxis(starts, 1, 0), state_end)


def assemble(y_intra, c_three, entry, carry, states, state_start):
    starts, state_end = span_fold(carry, states, state_start)
    y_full = y_intra + jnp.einsum("nci,hci,chpn->hpci", c_three, entry, starts, precision=precise)
    return (y_full.reshape(y_full.shape[0] * y_full.shape[1], -1), state_end)


def reach(carry):

    def reach_advance(product, factor):
        return (product * factor, product)

    total, before = lax.scan(
        reach_advance, jnp.ones(carry.shape[:-1], jnp.float32), jnp.moveaxis(carry, -1, 0)
    )
    return (jnp.moveaxis(before, 0, -1), total)


def shards(
    x_in, b_in, c_in, dt_raw, cotangent, conv_weight, conv_bias, dt_bias, a_log, d_skip, doc_lengths
):
    lane = lax.axis_index("seq")
    x_width = x_in.shape[1]
    n_heads = dt_raw.shape[1]
    length = x_in.shape[2]
    blocks = length // SPAN
    b_full = lax.all_gather(b_in, "seq", axis=1, tiled=True)
    c_full = lax.all_gather(c_in, "seq", axis=1, tiled=True)
    groups_held = conv_weight.shape[0]
    packed = jnp.concatenate(
        [
            conv_weight.reshape(groups_held, -1),
            conv_bias,
            dt_bias,
            a_log,
            d_skip,
        ],
        axis=1,
    )
    packed_all = lax.all_gather(packed, "head", axis=0, tiled=True)
    cuts = [conv_weight[0].size, conv_bias.shape[1], dt_bias.shape[1], a_log.shape[1]]
    bounds = [sum(cuts[:k]) for k in range(len(cuts) + 1)]
    weight_all = packed_all[:, : bounds[1]].reshape((-1,) + conv_weight.shape[1:])
    bias_all = packed_all[:, bounds[1] : bounds[2]]
    dt_bias_all = packed_all[:, bounds[2] : bounds[3]]
    a_log_all = packed_all[:, bounds[3] : bounds[4]]
    d_skip_all = packed_all[:, bounds[4] :]
    x_total = weight_all.shape[2] - 2 * STATE

    def own_channels(table):
        mine = lax.dynamic_slice_in_dim(table, lane * x_width, x_width, axis=table.ndim - 1)
        return jnp.concatenate([mine, table[..., x_total:]], axis=table.ndim - 1)

    weight_here = own_channels(weight_all)
    bias_here = own_channels(bias_all)
    dt_bias_here = lax.dynamic_slice_in_dim(dt_bias_all, lane * n_heads, n_heads, axis=1)
    a_log_here = lax.dynamic_slice_in_dim(a_log_all, lane * n_heads, n_heads, axis=1)
    d_skip_here = lax.dynamic_slice_in_dim(d_skip_all, lane * n_heads, n_heads, axis=1)
    groups_here = x_in.shape[0]
    raw_chan = jnp.concatenate([x_in, b_full, c_full], axis=1)
    rim_chan = passed_along(raw_chan[:, :, length - (TAPS - 1) :], "head", 1)
    rank = lax.axis_index("head")
    positions = rank * length + jnp.arange(-(TAPS - 1), length, dtype=jnp.int32)
    segment_extended = segment_ids(positions, doc_lengths)

    def local_terms(raw_float, rim_float, dt_float):
        return jax.vmap(group_terms, in_axes=(0, 0, 0, 0, 0, 0, 0, 0, None))(
            raw_float,
            rim_float,
            dt_float,
            weight_here,
            bias_here,
            dt_bias_here,
            a_log_here,
            d_skip_here,
            segment_extended,
        )

    terms, pull_terms = jax.vjp(
        local_terms,
        raw_chan.astype(jnp.float32),
        rim_chan.astype(jnp.float32),
        dt_raw.astype(jnp.float32),
    )
    y_intra, c_three, entry, carry, states = terms
    before, total = reach(carry)
    state_zero = jnp.zeros((groups_here, n_heads, HEAD_DIM, STATE), jnp.float32)
    _, summary = jax.vmap(span_fold)(carry, states, state_zero)
    state_in = carried_in(total, summary, "head", False)

    def finish(pieces, state_start):
        return jax.vmap(assemble)(
            pieces[0], pieces[1], pieces[2], pieces[3], pieces[4], state_start
        )

    (y_scan, state_out), pull_out = jax.vjp(finish, terms, state_in)
    y_out = y_scan.astype(jnp.bfloat16)
    cot_float = cotangent.astype(jnp.float32)
    cot_five = cot_float.reshape(groups_here, n_heads, HEAD_DIM, blocks, SPAN)
    local_grad = jnp.einsum(
        "ghpci,ghci,gnci->ghpn", cot_five, entry * before[..., None], c_three, precision=precise
    )
    grad_out = carried_in(total, local_grad, "head", True)
    d_terms, _ = pull_out((cot_float, grad_out))
    d_raw, d_rim, d_dt = pull_terms(d_terms)
    returned = passed_along(d_rim, "head", -1)
    cut_at = length - (TAPS - 1)
    d_raw = jnp.concatenate([d_raw[:, :, :cut_at], d_raw[:, :, cut_at:] + returned], axis=2)
    x_grad = d_raw[:, :x_width].astype(jnp.bfloat16)
    b_grad = lax.psum_scatter(
        d_raw[:, x_width : x_width + STATE], "seq", scatter_dimension=1, tiled=True
    ).astype(jnp.bfloat16)
    c_grad = lax.psum_scatter(
        d_raw[:, x_width + STATE :], "seq", scatter_dimension=1, tiled=True
    ).astype(jnp.bfloat16)
    dt_grad = d_dt.astype(jnp.bfloat16)
    return (y_out, x_grad, b_grad, c_grad, dt_grad)


def solution(mesh):
    return jax.shard_map(
        shards,
        mesh=mesh,
        in_specs=(
            P(None, "seq", "head"),
            P(None, "seq", "head"),
            P(None, "seq", "head"),
            P(None, "seq", "head"),
            P(None, "seq", "head"),
            P("head", None, None),
            P("head", None),
            P("head", None),
            P("head", None),
            P("head", None),
            P(),
        ),
        out_specs=(
            P(None, "seq", "head"),
            P(None, "seq", "head"),
            P(None, "seq", "head"),
            P(None, "seq", "head"),
            P(None, "seq", "head"),
        ),
        check_vma=False,
    )
```

```python
import jax
import jax.numpy as jnp
from jax import lax
from jax.sharding import PartitionSpec as P

HEAD_DIM = 64
STATE = 256
TAPS = 4
SPAN = 128


precise = lax.Precision.HIGHEST


def passed_along(value, axis, steps):
    count = lax.axis_size(axis)
    first, last = (max(0, -steps), min(count, count - steps))
    return lax.ppermute(value, axis, [(source, source + steps) for source in range(first, last)])


def carried_both(totals, ahead, behind, axis):
    factor = totals[..., None, None]
    pair = lax.optimization_barrier((ahead, behind))
    received = lax.optimization_barrier(
        (passed_along(pair[0], axis, 1), passed_along(pair[1], axis, -1))
    )
    for _ in range(lax.axis_size(axis) - 2):
        received = lax.optimization_barrier(
            (
                passed_along(factor * received[0] + ahead, axis, 1),
                passed_along(factor * received[1] + behind, axis, -1),
            )
        )
    return received


def segment_ids(positions, doc_lengths):
    ends = jnp.cumsum(doc_lengths)
    counted = jnp.sum((ends[None, :] <= positions[:, None]).astype(jnp.int32), axis=1)
    return jnp.where(positions >= 0, counted, -1)


def conv_silu(padded, weight, bias, segment_extended, length):
    total = jnp.zeros((padded.shape[0], length), jnp.float32) + bias[:, None]
    for offset in range(TAPS):
        same_doc = (
            segment_extended[offset : offset + length] == segment_extended[TAPS - 1 :]
        ).astype(jnp.float32)
        total = (
            total
            + weight[offset][:, None] * padded[:, offset : offset + length] * same_doc[None, :]
        )
    return jax.nn.silu(total)


def span_terms(x_conv, b_conv, c_conv, step_size, log_decay, seg_tok, seg_before, skip_gain):
    n_heads, length = step_size.shape
    blocks = length // SPAN
    x_four = x_conv.reshape(n_heads, HEAD_DIM, blocks, SPAN)
    b_three = b_conv.reshape(STATE, blocks, SPAN)
    c_three = c_conv.reshape(STATE, blocks, SPAN)
    step_three = step_size.reshape(n_heads, blocks, SPAN)
    seg_two = seg_tok.reshape(blocks, SPAN)
    rows_idx = lax.broadcasted_iota(jnp.int32, (SPAN, SPAN), 0)
    cols_idx = lax.broadcasted_iota(jnp.int32, (SPAN, SPAN), 1)
    lower = (rows_idx >= cols_idx).astype(jnp.float32)
    cumul = jnp.einsum(
        "hcj,ij->hci", log_decay.reshape(n_heads, blocks, SPAN), lower, precision=precise
    )
    mask_doc = lower[None] * (seg_two[:, :, None] == seg_two[:, None, :]).astype(jnp.float32)
    decay = jnp.exp(jnp.minimum(cumul[:, :, :, None] - cumul[:, :, None, :], 0.0)) * mask_doc[None]
    scores = jnp.einsum("nci,ncj->cij", c_three, b_three, precision=precise)
    weighted = x_four * step_three[:, None]
    y_intra = jnp.einsum("hcij,hpcj->hpci", decay * scores[None], weighted, precision=precise)
    y_intra = y_intra + skip_gain[:, None, None, None] * x_four
    last_cum = cumul[:, :, -1:]
    keep_end = jnp.exp(last_cum - cumul) * (seg_two == seg_two[:, -1:]).astype(jnp.float32)[None]
    states = jnp.einsum("hpcj,hcj,ncj->hcpn", weighted, keep_end, b_three, precision=precise)
    prev_seg = jnp.concatenate([seg_before[None], seg_two[:-1, -1]])
    entry = jnp.exp(cumul) * (seg_two == prev_seg[:, None]).astype(jnp.float32)[None]
    carry = jnp.exp(last_cum[:, :, 0]) * (seg_two[:, -1] == prev_seg).astype(jnp.float32)[None]
    return (y_intra, c_three, entry, carry, states)


def group_terms(
    raw_chan, rim_chan, dt_pre, weight, bias, bias_dt, log_rate, skip_gain, segment_extended
):
    n_heads = dt_pre.shape[0]
    length = raw_chan.shape[1]
    padded = jnp.concatenate([rim_chan, raw_chan], axis=1)
    active = conv_silu(padded, weight, bias, segment_extended, length)
    split_at = n_heads * HEAD_DIM
    x_conv = active[:split_at]
    b_conv = active[split_at : split_at + STATE]
    c_conv = active[split_at + STATE :]
    step_size = jax.nn.softplus(dt_pre + bias_dt[:, None])
    log_decay = step_size * (-jnp.exp(log_rate))[:, None]
    return span_terms(
        x_conv,
        b_conv,
        c_conv,
        step_size,
        log_decay,
        segment_extended[TAPS - 1 :],
        segment_extended[TAPS - 2],
        skip_gain,
    )


def weighted_sum(weight, stacked):
    return jnp.sum(weight[..., None, None] * stacked, axis=-3)


def span_fold(carry, states, state_start):
    blocks = carry.shape[-1]
    idx = jnp.arange(blocks)
    inside = (idx[None, :, None] < idx[None, None, :]) & (idx[None, None, :] < idx[:, None, None])
    link = jnp.prod(jnp.where(inside[None], carry[:, None, None, :], 1.0), axis=-1)
    link = link * (idx[None, :] < idx[:, None]).astype(jnp.float32)[None]
    lead = jnp.prod(jnp.where((idx[None, :] < idx[:, None])[None], carry[:, None, :], 1.0), axis=-1)
    tail = jnp.prod(jnp.where((idx[None, :] > idx[:, None])[None], carry[:, None, :], 1.0), axis=-1)
    starts = weighted_sum(link, states[:, None]) + lead[..., None, None] * state_start[:, None]
    state_end = weighted_sum(tail, states) + jnp.prod(carry, axis=-1)[:, None, None] * state_start
    return (jnp.moveaxis(starts, 1, 0), state_end)


def assemble(y_intra, c_three, entry, carry, states, state_start):
    starts, state_end = span_fold(carry, states, state_start)
    y_full = y_intra + jnp.einsum("nci,hci,chpn->hpci", c_three, entry, starts, precision=precise)
    return (y_full.reshape(y_full.shape[0] * y_full.shape[1], -1), state_end)


def reach(carry):

    def reach_advance(product, factor):
        return (product * factor, product)

    total, before = lax.scan(
        reach_advance, jnp.ones(carry.shape[:-1], jnp.float32), jnp.moveaxis(carry, -1, 0)
    )
    return (jnp.moveaxis(before, 0, -1), total)


def shards(
    x_in, b_in, c_in, dt_raw, cotangent, conv_weight, conv_bias, dt_bias, a_log, d_skip, doc_lengths
):
    lane = lax.axis_index("seq")
    x_width = x_in.shape[1]
    n_heads = dt_raw.shape[1]
    length = x_in.shape[2]
    blocks = length // SPAN
    b_full = lax.all_gather(b_in, "seq", axis=1, tiled=True)
    c_full = lax.all_gather(c_in, "seq", axis=1, tiled=True)
    groups_held = conv_weight.shape[0]
    packed = jnp.concatenate(
        [
            conv_weight.reshape(groups_held, -1),
            conv_bias,
            dt_bias,
            a_log,
            d_skip,
        ],
        axis=1,
    )
    packed_all = lax.all_gather(packed, "head", axis=0, tiled=True)
    cuts = [conv_weight[0].size, conv_bias.shape[1], dt_bias.shape[1], a_log.shape[1]]
    bounds = [sum(cuts[:k]) for k in range(len(cuts) + 1)]
    weight_all = packed_all[:, : bounds[1]].reshape((-1,) + conv_weight.shape[1:])
    bias_all = packed_all[:, bounds[1] : bounds[2]]
    dt_bias_all = packed_all[:, bounds[2] : bounds[3]]
    a_log_all = packed_all[:, bounds[3] : bounds[4]]
    d_skip_all = packed_all[:, bounds[4] :]
    x_total = weight_all.shape[2] - 2 * STATE

    def own_channels(table):
        mine = lax.dynamic_slice_in_dim(table, lane * x_width, x_width, axis=table.ndim - 1)
        return jnp.concatenate([mine, table[..., x_total:]], axis=table.ndim - 1)

    weight_here = own_channels(weight_all)
    bias_here = own_channels(bias_all)
    dt_bias_here = lax.dynamic_slice_in_dim(dt_bias_all, lane * n_heads, n_heads, axis=1)
    a_log_here = lax.dynamic_slice_in_dim(a_log_all, lane * n_heads, n_heads, axis=1)
    d_skip_here = lax.dynamic_slice_in_dim(d_skip_all, lane * n_heads, n_heads, axis=1)
    groups_here = x_in.shape[0]
    raw_chan = jnp.concatenate([x_in, b_full, c_full], axis=1)
    rim_chan = passed_along(raw_chan[:, :, length - (TAPS - 1) :], "head", 1)
    rank = lax.axis_index("head")
    positions = rank * length + jnp.arange(-(TAPS - 1), length, dtype=jnp.int32)
    segment_extended = segment_ids(positions, doc_lengths)

    def local_terms(raw_float, rim_float, dt_float):
        return jax.vmap(group_terms, in_axes=(0, 0, 0, 0, 0, 0, 0, 0, None))(
            raw_float,
            rim_float,
            dt_float,
            weight_here,
            bias_here,
            dt_bias_here,
            a_log_here,
            d_skip_here,
            segment_extended,
        )

    terms, pull_terms = jax.vjp(
        local_terms,
        raw_chan.astype(jnp.float32),
        rim_chan.astype(jnp.float32),
        dt_raw.astype(jnp.float32),
    )
    y_intra, c_three, entry, carry, states = terms
    before, total = reach(carry)
    state_zero = jnp.zeros((groups_here, n_heads, HEAD_DIM, STATE), jnp.float32)
    _, summary = jax.vmap(span_fold)(carry, states, state_zero)
    cot_float = cotangent.astype(jnp.float32)
    cot_five = cot_float.reshape(groups_here, n_heads, HEAD_DIM, blocks, SPAN)
    local_grad = jnp.einsum(
        "ghpci,ghci,gnci->ghpn", cot_five, entry * before[..., None], c_three, precision=precise
    )
    state_in, grad_out = carried_both(total, summary, local_grad, "head")

    def finish(pieces, state_start):
        return jax.vmap(assemble)(
            pieces[0], pieces[1], pieces[2], pieces[3], pieces[4], state_start
        )

    (y_scan, state_out), pull_out = jax.vjp(finish, terms, state_in)
    y_out = y_scan.astype(jnp.bfloat16)
    d_terms, _ = pull_out((cot_float, grad_out))
    d_raw, d_rim, d_dt = pull_terms(d_terms)
    returned = passed_along(d_rim, "head", -1)
    cut_at = length - (TAPS - 1)
    d_raw = jnp.concatenate([d_raw[:, :, :cut_at], d_raw[:, :, cut_at:] + returned], axis=2)
    x_grad = d_raw[:, :x_width].astype(jnp.bfloat16)
    b_grad = lax.psum_scatter(
        d_raw[:, x_width : x_width + STATE], "seq", scatter_dimension=1, tiled=True
    ).astype(jnp.bfloat16)
    c_grad = lax.psum_scatter(
        d_raw[:, x_width + STATE :], "seq", scatter_dimension=1, tiled=True
    ).astype(jnp.bfloat16)
    dt_grad = d_dt.astype(jnp.bfloat16)
    return (y_out, x_grad, b_grad, c_grad, dt_grad)


def solution(mesh):
    return jax.shard_map(
        shards,
        mesh=mesh,
        in_specs=(
            P(None, "seq", "head"),
            P(None, "seq", "head"),
            P(None, "seq", "head"),
            P(None, "seq", "head"),
            P(None, "seq", "head"),
            P("head", None, None),
            P("head", None),
            P("head", None),
            P("head", None),
            P("head", None),
            P(),
        ),
        out_specs=(
            P(None, "seq", "head"),
            P(None, "seq", "head"),
            P(None, "seq", "head"),
            P(None, "seq", "head"),
            P(None, "seq", "head"),
        ),
        check_vma=False,
    )
```

```python
import jax
import jax.numpy as jnp
from jax import lax
from jax.sharding import PartitionSpec as P

HEAD_DIM = 64
STATE = 256
TAPS = 4
SPAN = 128


precise = lax.Precision.HIGHEST


def passed_along(value, axis, steps):
    count = lax.axis_size(axis)
    first, last = (max(0, -steps), min(count, count - steps))
    return lax.ppermute(value, axis, [(source, source + steps) for source in range(first, last)])


def carried_both(totals, ahead, behind, axis):
    factor = totals[..., None, None]
    pair = lax.optimization_barrier((ahead, behind))
    received = lax.optimization_barrier(
        (passed_along(pair[0], axis, 1), passed_along(pair[1], axis, -1))
    )
    for _ in range(lax.axis_size(axis) - 2):
        received = lax.optimization_barrier(
            (
                passed_along(factor * received[0] + ahead, axis, 1),
                passed_along(factor * received[1] + behind, axis, -1),
            )
        )
    return received


def segment_ids(positions, doc_lengths):
    ends = jnp.cumsum(doc_lengths)
    counted = jnp.sum((ends[None, :] <= positions[:, None]).astype(jnp.int32), axis=1)
    return jnp.where(positions >= 0, counted, -1)


def conv_silu(padded, weight, bias, segment_extended, length):
    total = jnp.zeros((padded.shape[0], length), jnp.float32) + bias[:, None]
    for offset in range(TAPS):
        same_doc = (
            segment_extended[offset : offset + length] == segment_extended[TAPS - 1 :]
        ).astype(jnp.float32)
        total = (
            total
            + weight[offset][:, None] * padded[:, offset : offset + length] * same_doc[None, :]
        )
    return jax.nn.silu(total)


def span_terms(x_conv, b_conv, c_conv, step_size, log_decay, seg_tok, seg_before, skip_gain):
    n_heads, length = step_size.shape
    blocks = length // SPAN
    x_four = x_conv.reshape(n_heads, HEAD_DIM, blocks, SPAN)
    b_three = b_conv.reshape(STATE, blocks, SPAN)
    c_three = c_conv.reshape(STATE, blocks, SPAN)
    step_three = step_size.reshape(n_heads, blocks, SPAN)
    seg_two = seg_tok.reshape(blocks, SPAN)
    rows_idx = lax.broadcasted_iota(jnp.int32, (SPAN, SPAN), 0)
    cols_idx = lax.broadcasted_iota(jnp.int32, (SPAN, SPAN), 1)
    lower = (rows_idx >= cols_idx).astype(jnp.float32)
    cumul = jnp.einsum(
        "hcj,ij->hci", log_decay.reshape(n_heads, blocks, SPAN), lower, precision=precise
    )
    mask_doc = lower[None] * (seg_two[:, :, None] == seg_two[:, None, :]).astype(jnp.float32)
    decay = jnp.exp(jnp.minimum(cumul[:, :, :, None] - cumul[:, :, None, :], 0.0)) * mask_doc[None]
    scores = jnp.einsum("nci,ncj->cij", c_three, b_three, precision=precise)
    weighted = x_four * step_three[:, None]
    y_intra = jnp.einsum("hcij,hpcj->hpci", decay * scores[None], weighted, precision=precise)
    y_intra = y_intra + skip_gain[:, None, None, None] * x_four
    last_cum = cumul[:, :, -1:]
    keep_end = jnp.exp(last_cum - cumul) * (seg_two == seg_two[:, -1:]).astype(jnp.float32)[None]
    states = jnp.einsum("hpcj,hcj,ncj->hcpn", weighted, keep_end, b_three, precision=precise)
    prev_seg = jnp.concatenate([seg_before[None], seg_two[:-1, -1]])
    entry = jnp.exp(cumul) * (seg_two == prev_seg[:, None]).astype(jnp.float32)[None]
    carry = jnp.exp(last_cum[:, :, 0]) * (seg_two[:, -1] == prev_seg).astype(jnp.float32)[None]
    return (y_intra, c_three, entry, carry, states)


def group_terms(
    raw_chan, rim_chan, dt_pre, weight, bias, bias_dt, log_rate, skip_gain, segment_extended
):
    n_heads = dt_pre.shape[0]
    length = raw_chan.shape[1]
    padded = jnp.concatenate([rim_chan, raw_chan], axis=1)
    active = conv_silu(padded, weight, bias, segment_extended, length)
    split_at = n_heads * HEAD_DIM
    x_conv = active[:split_at]
    b_conv = active[split_at : split_at + STATE]
    c_conv = active[split_at + STATE :]
    step_size = jax.nn.softplus(dt_pre + bias_dt[:, None])
    log_decay = step_size * (-jnp.exp(log_rate))[:, None]
    return span_terms(
        x_conv,
        b_conv,
        c_conv,
        step_size,
        log_decay,
        segment_extended[TAPS - 1 :],
        segment_extended[TAPS - 2],
        skip_gain,
    )


def conv_part(raw_chan, rim_chan, weight, bias, segment_extended):
    padded = jnp.concatenate([rim_chan, raw_chan], axis=1)
    return conv_silu(padded, weight, bias, segment_extended, raw_chan.shape[1])


def scan_part(x_conv, b_conv, c_conv, dt_pre, bias_dt, log_rate, skip_gain, segment_extended):
    step_size = jax.nn.softplus(dt_pre + bias_dt[:, None])
    log_decay = step_size * (-jnp.exp(log_rate))[:, None]
    return span_terms(
        x_conv,
        b_conv,
        c_conv,
        step_size,
        log_decay,
        segment_extended[TAPS - 1 :],
        segment_extended[TAPS - 2],
        skip_gain,
    )


def weighted_sum(weight, stacked):
    return jnp.sum(weight[..., None, None] * stacked, axis=-3)


def span_fold(carry, states, state_start):
    blocks = carry.shape[-1]
    idx = jnp.arange(blocks)
    inside = (idx[None, :, None] < idx[None, None, :]) & (idx[None, None, :] < idx[:, None, None])
    link = jnp.prod(jnp.where(inside[None], carry[:, None, None, :], 1.0), axis=-1)
    link = link * (idx[None, :] < idx[:, None]).astype(jnp.float32)[None]
    lead = jnp.prod(jnp.where((idx[None, :] < idx[:, None])[None], carry[:, None, :], 1.0), axis=-1)
    tail = jnp.prod(jnp.where((idx[None, :] > idx[:, None])[None], carry[:, None, :], 1.0), axis=-1)
    starts = weighted_sum(link, states[:, None]) + lead[..., None, None] * state_start[:, None]
    state_end = weighted_sum(tail, states) + jnp.prod(carry, axis=-1)[:, None, None] * state_start
    return (jnp.moveaxis(starts, 1, 0), state_end)


def assemble(y_intra, c_three, entry, carry, states, state_start):
    starts, state_end = span_fold(carry, states, state_start)
    y_full = y_intra + jnp.einsum("nci,hci,chpn->hpci", c_three, entry, starts, precision=precise)
    return (y_full.reshape(y_full.shape[0] * y_full.shape[1], -1), state_end)


def reach(carry):

    def reach_advance(product, factor):
        return (product * factor, product)

    total, before = lax.scan(
        reach_advance, jnp.ones(carry.shape[:-1], jnp.float32), jnp.moveaxis(carry, -1, 0)
    )
    return (jnp.moveaxis(before, 0, -1), total)


def shards(
    x_in, b_in, c_in, dt_raw, cotangent, conv_weight, conv_bias, dt_bias, a_log, d_skip, doc_lengths
):
    lane = lax.axis_index("seq")
    x_width = x_in.shape[1]
    n_heads = dt_raw.shape[1]
    length = x_in.shape[2]
    blocks = length // SPAN
    groups_held = conv_weight.shape[0]
    packed = jnp.concatenate(
        [
            conv_weight.reshape(groups_held, -1),
            conv_bias,
            dt_bias,
            a_log,
            d_skip,
        ],
        axis=1,
    )
    packed_all = lax.all_gather(packed, "head", axis=0, tiled=True)
    cuts = [conv_weight[0].size, conv_bias.shape[1], dt_bias.shape[1], a_log.shape[1]]
    bounds = [sum(cuts[:k]) for k in range(len(cuts) + 1)]
    weight_all = packed_all[:, : bounds[1]].reshape((-1,) + conv_weight.shape[1:])
    bias_all = packed_all[:, bounds[1] : bounds[2]]
    dt_bias_all = packed_all[:, bounds[2] : bounds[3]]
    a_log_all = packed_all[:, bounds[3] : bounds[4]]
    d_skip_all = packed_all[:, bounds[4] :]
    x_total = weight_all.shape[2] - 2 * STATE

    b_width = b_in.shape[1]

    def own_channels(table):
        pieces = [
            lax.dynamic_slice_in_dim(table, start + lane * width, width, axis=table.ndim - 1)
            for start, width in ((0, x_width), (x_total, b_width), (x_total + STATE, b_width))
        ]
        return (pieces[0], jnp.concatenate(pieces[1:], axis=table.ndim - 1))

    weight_x, weight_bc = own_channels(weight_all)
    bias_x, bias_bc = own_channels(bias_all)
    dt_bias_here = lax.dynamic_slice_in_dim(dt_bias_all, lane * n_heads, n_heads, axis=1)
    a_log_here = lax.dynamic_slice_in_dim(a_log_all, lane * n_heads, n_heads, axis=1)
    d_skip_here = lax.dynamic_slice_in_dim(d_skip_all, lane * n_heads, n_heads, axis=1)
    groups_here = x_in.shape[0]
    raw_chan = jnp.concatenate([x_in, b_in, c_in], axis=1)
    rim_chan = passed_along(raw_chan[:, :, length - (TAPS - 1) :], "head", 1)
    rank = lax.axis_index("head")
    positions = rank * length + jnp.arange(-(TAPS - 1), length, dtype=jnp.int32)
    segment_extended = segment_ids(positions, doc_lengths)
    each_group = (0, 0, 0, 0, None)

    def own_conv(x_float, bc_float, rim_float):
        x_conv = jax.vmap(conv_part, in_axes=each_group)(
            x_float, rim_float[:, :x_width], weight_x, bias_x, segment_extended
        )
        bc_conv = jax.vmap(conv_part, in_axes=each_group)(
            bc_float, rim_float[:, x_width:], weight_bc, bias_bc, segment_extended
        )
        return (x_conv, bc_conv)

    (x_conv, bc_conv), pull_conv = jax.vjp(
        own_conv,
        x_in.astype(jnp.float32),
        jnp.concatenate([b_in, c_in], axis=1).astype(jnp.float32),
        rim_chan.astype(jnp.float32),
    )
    b_conv = lax.all_gather(bc_conv[:, :b_width], "seq", axis=1, tiled=True)
    c_conv = lax.all_gather(bc_conv[:, b_width:], "seq", axis=1, tiled=True)

    def local_terms(x_float, b_float, c_float, dt_float):
        return jax.vmap(scan_part, in_axes=(0, 0, 0, 0, 0, 0, 0, None))(
            x_float,
            b_float,
            c_float,
            dt_float,
            dt_bias_here,
            a_log_here,
            d_skip_here,
            segment_extended,
        )

    terms, pull_terms = jax.vjp(local_terms, x_conv, b_conv, c_conv, dt_raw.astype(jnp.float32))
    y_intra, c_three, entry, carry, states = terms
    before, total = reach(carry)
    state_zero = jnp.zeros((groups_here, n_heads, HEAD_DIM, STATE), jnp.float32)
    _, summary = jax.vmap(span_fold)(carry, states, state_zero)
    cot_float = cotangent.astype(jnp.float32)
    cot_five = cot_float.reshape(groups_here, n_heads, HEAD_DIM, blocks, SPAN)
    local_grad = jnp.einsum(
        "ghpci,ghci,gnci->ghpn", cot_five, entry * before[..., None], c_three, precision=precise
    )
    state_in, grad_out = carried_both(total, summary, local_grad, "head")

    def finish(pieces, state_start):
        return jax.vmap(assemble)(
            pieces[0], pieces[1], pieces[2], pieces[3], pieces[4], state_start
        )

    (y_scan, state_out), pull_out = jax.vjp(finish, terms, state_in)
    y_out = y_scan.astype(jnp.bfloat16)
    d_terms, _ = pull_out((cot_float, grad_out))
    d_x_conv, d_b_conv, d_c_conv, d_dt = pull_terms(d_terms)
    d_bc_conv = jnp.concatenate(
        [
            lax.psum_scatter(d_b_conv, "seq", scatter_dimension=1, tiled=True),
            lax.psum_scatter(d_c_conv, "seq", scatter_dimension=1, tiled=True),
        ],
        axis=1,
    )
    d_x, d_bc, d_rim = pull_conv((d_x_conv, d_bc_conv))
    d_raw = jnp.concatenate([d_x, d_bc], axis=1)
    returned = passed_along(d_rim, "head", -1)
    cut_at = length - (TAPS - 1)
    d_raw = jnp.concatenate([d_raw[:, :, :cut_at], d_raw[:, :, cut_at:] + returned], axis=2)
    x_grad = d_raw[:, :x_width].astype(jnp.bfloat16)
    b_grad = d_raw[:, x_width : x_width + b_width].astype(jnp.bfloat16)
    c_grad = d_raw[:, x_width + b_width :].astype(jnp.bfloat16)
    dt_grad = d_dt.astype(jnp.bfloat16)
    return (y_out, x_grad, b_grad, c_grad, dt_grad)


def solution(mesh):
    return jax.shard_map(
        shards,
        mesh=mesh,
        in_specs=(
            P(None, "seq", "head"),
            P(None, "seq", "head"),
            P(None, "seq", "head"),
            P(None, "seq", "head"),
            P(None, "seq", "head"),
            P("head", None, None),
            P("head", None),
            P("head", None),
            P("head", None),
            P("head", None),
            P(),
        ),
        out_specs=(
            P(None, "seq", "head"),
            P(None, "seq", "head"),
            P(None, "seq", "head"),
            P(None, "seq", "head"),
            P(None, "seq", "head"),
        ),
        check_vma=False,
    )
```

```python
import jax
import jax.numpy as jnp
from jax import lax
from jax.sharding import PartitionSpec as P

HEAD_DIM = 64
STATE = 256
TAPS = 4
SPAN = 128


precise = lax.Precision.HIGHEST


def passed_along(value, axis, steps):
    count = lax.axis_size(axis)
    first, last = (max(0, -steps), min(count, count - steps))
    return lax.ppermute(value, axis, [(source, source + steps) for source in range(first, last)])


def carried_both(totals, ahead, behind, axis, chunks=2):
    hops = lax.axis_size(axis) - 1
    size = totals.shape[0] // chunks
    part = lambda value, c: value[c * size : (c + 1) * size]
    factor = [part(totals, c)[..., None, None] for c in range(chunks)]
    ahead, behind = lax.optimization_barrier((ahead, behind))
    own = [(part(ahead, c), part(behind, c)) for c in range(chunks)]
    received = [None] * chunks
    for step in range(hops + chunks - 1):
        sent = {}
        for c in range(chunks):
            hop = step - c
            if 0 <= hop < hops:
                if hop == 0:
                    values = own[c]
                else:
                    values = tuple(factor[c] * r + o for r, o in zip(received[c], own[c]))
                sent[c] = (passed_along(values[0], axis, 1), passed_along(values[1], axis, -1))
        sent = lax.optimization_barrier(sent)
        for c, values in sent.items():
            received[c] = values
    return tuple(jnp.concatenate([received[c][k] for c in range(chunks)], axis=0) for k in range(2))


def segment_ids(positions, doc_lengths):
    ends = jnp.cumsum(doc_lengths)
    counted = jnp.sum((ends[None, :] <= positions[:, None]).astype(jnp.int32), axis=1)
    return jnp.where(positions >= 0, counted, -1)


def conv_silu(padded, weight, bias, segment_extended, length):
    total = jnp.zeros((padded.shape[0], length), jnp.float32) + bias[:, None]
    for offset in range(TAPS):
        same_doc = (
            segment_extended[offset : offset + length] == segment_extended[TAPS - 1 :]
        ).astype(jnp.float32)
        total = (
            total
            + weight[offset][:, None] * padded[:, offset : offset + length] * same_doc[None, :]
        )
    return jax.nn.silu(total)


def span_terms(x_conv, b_conv, c_conv, step_size, log_decay, seg_tok, seg_before, skip_gain):
    n_heads, length = step_size.shape
    blocks = length // SPAN
    x_four = x_conv.reshape(n_heads, HEAD_DIM, blocks, SPAN)
    b_three = b_conv.reshape(STATE, blocks, SPAN)
    c_three = c_conv.reshape(STATE, blocks, SPAN)
    step_three = step_size.reshape(n_heads, blocks, SPAN)
    seg_two = seg_tok.reshape(blocks, SPAN)
    rows_idx = lax.broadcasted_iota(jnp.int32, (SPAN, SPAN), 0)
    cols_idx = lax.broadcasted_iota(jnp.int32, (SPAN, SPAN), 1)
    lower = (rows_idx >= cols_idx).astype(jnp.float32)
    cumul = jnp.einsum(
        "hcj,ij->hci", log_decay.reshape(n_heads, blocks, SPAN), lower, precision=precise
    )
    mask_doc = lower[None] * (seg_two[:, :, None] == seg_two[:, None, :]).astype(jnp.float32)
    decay = jnp.exp(jnp.minimum(cumul[:, :, :, None] - cumul[:, :, None, :], 0.0)) * mask_doc[None]
    scores = jnp.einsum("nci,ncj->cij", c_three, b_three, precision=precise)
    weighted = x_four * step_three[:, None]
    y_intra = jnp.einsum("hcij,hpcj->hpci", decay * scores[None], weighted, precision=precise)
    y_intra = y_intra + skip_gain[:, None, None, None] * x_four
    last_cum = cumul[:, :, -1:]
    keep_end = jnp.exp(last_cum - cumul) * (seg_two == seg_two[:, -1:]).astype(jnp.float32)[None]
    states = jnp.einsum("hpcj,hcj,ncj->hcpn", weighted, keep_end, b_three, precision=precise)
    prev_seg = jnp.concatenate([seg_before[None], seg_two[:-1, -1]])
    entry = jnp.exp(cumul) * (seg_two == prev_seg[:, None]).astype(jnp.float32)[None]
    carry = jnp.exp(last_cum[:, :, 0]) * (seg_two[:, -1] == prev_seg).astype(jnp.float32)[None]
    return (y_intra, c_three, entry, carry, states)


def group_terms(
    raw_chan, rim_chan, dt_pre, weight, bias, bias_dt, log_rate, skip_gain, segment_extended
):
    n_heads = dt_pre.shape[0]
    length = raw_chan.shape[1]
    padded = jnp.concatenate([rim_chan, raw_chan], axis=1)
    active = conv_silu(padded, weight, bias, segment_extended, length)
    split_at = n_heads * HEAD_DIM
    x_conv = active[:split_at]
    b_conv = active[split_at : split_at + STATE]
    c_conv = active[split_at + STATE :]
    step_size = jax.nn.softplus(dt_pre + bias_dt[:, None])
    log_decay = step_size * (-jnp.exp(log_rate))[:, None]
    return span_terms(
        x_conv,
        b_conv,
        c_conv,
        step_size,
        log_decay,
        segment_extended[TAPS - 1 :],
        segment_extended[TAPS - 2],
        skip_gain,
    )


def conv_part(raw_chan, rim_chan, weight, bias, segment_extended):
    padded = jnp.concatenate([rim_chan, raw_chan], axis=1)
    return conv_silu(padded, weight, bias, segment_extended, raw_chan.shape[1])


def scan_part(x_conv, b_conv, c_conv, dt_pre, bias_dt, log_rate, skip_gain, segment_extended):
    step_size = jax.nn.softplus(dt_pre + bias_dt[:, None])
    log_decay = step_size * (-jnp.exp(log_rate))[:, None]
    return span_terms(
        x_conv,
        b_conv,
        c_conv,
        step_size,
        log_decay,
        segment_extended[TAPS - 1 :],
        segment_extended[TAPS - 2],
        skip_gain,
    )


def weighted_sum(weight, stacked):
    return jnp.sum(weight[..., None, None] * stacked, axis=-3)


def span_fold(carry, states, state_start):
    blocks = carry.shape[-1]
    idx = jnp.arange(blocks)
    inside = (idx[None, :, None] < idx[None, None, :]) & (idx[None, None, :] < idx[:, None, None])
    link = jnp.prod(jnp.where(inside[None], carry[:, None, None, :], 1.0), axis=-1)
    link = link * (idx[None, :] < idx[:, None]).astype(jnp.float32)[None]
    lead = jnp.prod(jnp.where((idx[None, :] < idx[:, None])[None], carry[:, None, :], 1.0), axis=-1)
    tail = jnp.prod(jnp.where((idx[None, :] > idx[:, None])[None], carry[:, None, :], 1.0), axis=-1)
    starts = weighted_sum(link, states[:, None]) + lead[..., None, None] * state_start[:, None]
    state_end = weighted_sum(tail, states) + jnp.prod(carry, axis=-1)[:, None, None] * state_start
    return (jnp.moveaxis(starts, 1, 0), state_end)


def assemble(y_intra, c_three, entry, carry, states, state_start):
    starts, state_end = span_fold(carry, states, state_start)
    y_full = y_intra + jnp.einsum("nci,hci,chpn->hpci", c_three, entry, starts, precision=precise)
    return (y_full.reshape(y_full.shape[0] * y_full.shape[1], -1), state_end)


def reach(carry):

    def reach_advance(product, factor):
        return (product * factor, product)

    total, before = lax.scan(
        reach_advance, jnp.ones(carry.shape[:-1], jnp.float32), jnp.moveaxis(carry, -1, 0)
    )
    return (jnp.moveaxis(before, 0, -1), total)


def shards(
    x_in, b_in, c_in, dt_raw, cotangent, conv_weight, conv_bias, dt_bias, a_log, d_skip, doc_lengths
):
    lane = lax.axis_index("seq")
    x_width = x_in.shape[1]
    n_heads = dt_raw.shape[1]
    length = x_in.shape[2]
    blocks = length // SPAN
    groups_held = conv_weight.shape[0]
    packed = jnp.concatenate(
        [
            conv_weight.reshape(groups_held, -1),
            conv_bias,
            dt_bias,
            a_log,
            d_skip,
        ],
        axis=1,
    )
    packed_all = lax.all_gather(packed, "head", axis=0, tiled=True)
    cuts = [conv_weight[0].size, conv_bias.shape[1], dt_bias.shape[1], a_log.shape[1]]
    bounds = [sum(cuts[:k]) for k in range(len(cuts) + 1)]
    weight_all = packed_all[:, : bounds[1]].reshape((-1,) + conv_weight.shape[1:])
    bias_all = packed_all[:, bounds[1] : bounds[2]]
    dt_bias_all = packed_all[:, bounds[2] : bounds[3]]
    a_log_all = packed_all[:, bounds[3] : bounds[4]]
    d_skip_all = packed_all[:, bounds[4] :]
    x_total = weight_all.shape[2] - 2 * STATE

    b_width = b_in.shape[1]

    def own_channels(table):
        pieces = [
            lax.dynamic_slice_in_dim(table, start + lane * width, width, axis=table.ndim - 1)
            for start, width in ((0, x_width), (x_total, b_width), (x_total + STATE, b_width))
        ]
        return (pieces[0], jnp.concatenate(pieces[1:], axis=table.ndim - 1))

    weight_x, weight_bc = own_channels(weight_all)
    bias_x, bias_bc = own_channels(bias_all)
    dt_bias_here = lax.dynamic_slice_in_dim(dt_bias_all, lane * n_heads, n_heads, axis=1)
    a_log_here = lax.dynamic_slice_in_dim(a_log_all, lane * n_heads, n_heads, axis=1)
    d_skip_here = lax.dynamic_slice_in_dim(d_skip_all, lane * n_heads, n_heads, axis=1)
    groups_here = x_in.shape[0]
    raw_chan = jnp.concatenate([x_in, b_in, c_in], axis=1)
    rim_chan = passed_along(raw_chan[:, :, length - (TAPS - 1) :], "head", 1)
    rank = lax.axis_index("head")
    positions = rank * length + jnp.arange(-(TAPS - 1), length, dtype=jnp.int32)
    segment_extended = segment_ids(positions, doc_lengths)
    each_group = (0, 0, 0, 0, None)

    def own_conv(x_float, bc_float, rim_float):
        x_conv = jax.vmap(conv_part, in_axes=each_group)(
            x_float, rim_float[:, :x_width], weight_x, bias_x, segment_extended
        )
        bc_conv = jax.vmap(conv_part, in_axes=each_group)(
            bc_float, rim_float[:, x_width:], weight_bc, bias_bc, segment_extended
        )
        return (x_conv, bc_conv)

    (x_conv, bc_conv), pull_conv = jax.vjp(
        own_conv,
        x_in.astype(jnp.float32),
        jnp.concatenate([b_in, c_in], axis=1).astype(jnp.float32),
        rim_chan.astype(jnp.float32),
    )
    b_conv = lax.all_gather(bc_conv[:, :b_width], "seq", axis=1, tiled=True)
    c_conv = lax.all_gather(bc_conv[:, b_width:], "seq", axis=1, tiled=True)

    def local_terms(x_float, b_float, c_float, dt_float):
        return jax.vmap(scan_part, in_axes=(0, 0, 0, 0, 0, 0, 0, None))(
            x_float,
            b_float,
            c_float,
            dt_float,
            dt_bias_here,
            a_log_here,
            d_skip_here,
            segment_extended,
        )

    terms, pull_terms = jax.vjp(local_terms, x_conv, b_conv, c_conv, dt_raw.astype(jnp.float32))
    y_intra, c_three, entry, carry, states = terms
    before, total = reach(carry)
    state_zero = jnp.zeros((groups_here, n_heads, HEAD_DIM, STATE), jnp.float32)
    _, summary = jax.vmap(span_fold)(carry, states, state_zero)
    cot_float = cotangent.astype(jnp.float32)
    cot_five = cot_float.reshape(groups_here, n_heads, HEAD_DIM, blocks, SPAN)
    local_grad = jnp.einsum(
        "ghpci,ghci,gnci->ghpn", cot_five, entry * before[..., None], c_three, precision=precise
    )
    state_in, grad_out = carried_both(total, summary, local_grad, "head")

    def finish(pieces, state_start):
        return jax.vmap(assemble)(
            pieces[0], pieces[1], pieces[2], pieces[3], pieces[4], state_start
        )

    (y_scan, state_out), pull_out = jax.vjp(finish, terms, state_in)
    y_out = y_scan.astype(jnp.bfloat16)
    d_terms, _ = pull_out((cot_float, grad_out))
    d_x_conv, d_b_conv, d_c_conv, d_dt = pull_terms(d_terms)
    d_bc_conv = jnp.concatenate(
        [
            lax.psum_scatter(d_b_conv, "seq", scatter_dimension=1, tiled=True),
            lax.psum_scatter(d_c_conv, "seq", scatter_dimension=1, tiled=True),
        ],
        axis=1,
    )
    d_x, d_bc, d_rim = pull_conv((d_x_conv, d_bc_conv))
    d_raw = jnp.concatenate([d_x, d_bc], axis=1)
    returned = passed_along(d_rim, "head", -1)
    cut_at = length - (TAPS - 1)
    d_raw = jnp.concatenate([d_raw[:, :, :cut_at], d_raw[:, :, cut_at:] + returned], axis=2)
    x_grad = d_raw[:, :x_width].astype(jnp.bfloat16)
    b_grad = d_raw[:, x_width : x_width + b_width].astype(jnp.bfloat16)
    c_grad = d_raw[:, x_width + b_width :].astype(jnp.bfloat16)
    dt_grad = d_dt.astype(jnp.bfloat16)
    return (y_out, x_grad, b_grad, c_grad, dt_grad)


def solution(mesh):
    return jax.shard_map(
        shards,
        mesh=mesh,
        in_specs=(
            P(None, "seq", "head"),
            P(None, "seq", "head"),
            P(None, "seq", "head"),
            P(None, "seq", "head"),
            P(None, "seq", "head"),
            P("head", None, None),
            P("head", None),
            P("head", None),
            P("head", None),
            P("head", None),
            P(),
        ),
        out_specs=(
            P(None, "seq", "head"),
            P(None, "seq", "head"),
            P(None, "seq", "head"),
            P(None, "seq", "head"),
            P(None, "seq", "head"),
        ),
        check_vma=False,
    )
```

```python
import jax
import jax.numpy as jnp
from jax import lax
from jax.sharding import PartitionSpec as P

HEAD_DIM = 64
STATE = 256
TAPS = 4
SPAN = 128


precise = lax.Precision.HIGHEST


def passed_along(value, axis, steps):
    count = lax.axis_size(axis)
    first, last = (max(0, -steps), min(count, count - steps))
    return lax.ppermute(value, axis, [(source, source + steps) for source in range(first, last)])


def carried_both(totals, ahead, behind, axis):
    factor = totals[..., None, None]
    pair = lax.optimization_barrier((ahead, behind))
    received = lax.optimization_barrier(
        (passed_along(pair[0], axis, 1), passed_along(pair[1], axis, -1))
    )
    for _ in range(lax.axis_size(axis) - 2):
        received = lax.optimization_barrier(
            (
                passed_along(factor * received[0] + ahead, axis, 1),
                passed_along(factor * received[1] + behind, axis, -1),
            )
        )
    return received


def segment_ids(positions, doc_lengths):
    ends = jnp.cumsum(doc_lengths)
    counted = jnp.sum((ends[None, :] <= positions[:, None]).astype(jnp.int32), axis=1)
    return jnp.where(positions >= 0, counted, -1)


def conv_silu(padded, weight, bias, segment_extended, length):
    total = jnp.zeros((padded.shape[0], length), jnp.float32) + bias[:, None]
    for offset in range(TAPS):
        same_doc = (
            segment_extended[offset : offset + length] == segment_extended[TAPS - 1 :]
        ).astype(jnp.float32)
        total = (
            total
            + weight[offset][:, None] * padded[:, offset : offset + length] * same_doc[None, :]
        )
    return jax.nn.silu(total)


def span_terms(x_conv, b_conv, c_conv, step_size, log_decay, seg_tok, seg_before, skip_gain):
    n_heads, length = step_size.shape
    blocks = length // SPAN
    x_four = x_conv.reshape(n_heads, HEAD_DIM, blocks, SPAN)
    b_three = b_conv.reshape(STATE, blocks, SPAN)
    c_three = c_conv.reshape(STATE, blocks, SPAN)
    step_three = step_size.reshape(n_heads, blocks, SPAN)
    seg_two = seg_tok.reshape(blocks, SPAN)
    rows_idx = lax.broadcasted_iota(jnp.int32, (SPAN, SPAN), 0)
    cols_idx = lax.broadcasted_iota(jnp.int32, (SPAN, SPAN), 1)
    lower = (rows_idx >= cols_idx).astype(jnp.float32)
    cumul = jnp.einsum(
        "hcj,ij->hci", log_decay.reshape(n_heads, blocks, SPAN), lower, precision=precise
    )
    mask_doc = lower[None] * (seg_two[:, :, None] == seg_two[:, None, :]).astype(jnp.float32)
    decay = jnp.exp(jnp.minimum(cumul[:, :, :, None] - cumul[:, :, None, :], 0.0)) * mask_doc[None]
    scores = jnp.einsum("nci,ncj->cij", c_three, b_three, precision=precise)
    weighted = x_four * step_three[:, None]
    y_intra = jnp.einsum("hcij,hpcj->hpci", decay * scores[None], weighted, precision=precise)
    y_intra = y_intra + skip_gain[:, None, None, None] * x_four
    last_cum = cumul[:, :, -1:]
    keep_end = jnp.exp(last_cum - cumul) * (seg_two == seg_two[:, -1:]).astype(jnp.float32)[None]
    states = jnp.einsum("hpcj,hcj,ncj->hcpn", weighted, keep_end, b_three, precision=precise)
    prev_seg = jnp.concatenate([seg_before[None], seg_two[:-1, -1]])
    entry = jnp.exp(cumul) * (seg_two == prev_seg[:, None]).astype(jnp.float32)[None]
    carry = jnp.exp(last_cum[:, :, 0]) * (seg_two[:, -1] == prev_seg).astype(jnp.float32)[None]
    return (y_intra, c_three, entry, carry, states)


def group_terms(
    raw_chan, rim_chan, dt_pre, weight, bias, bias_dt, log_rate, skip_gain, segment_extended
):
    n_heads = dt_pre.shape[0]
    length = raw_chan.shape[1]
    padded = jnp.concatenate([rim_chan, raw_chan], axis=1)
    active = conv_silu(padded, weight, bias, segment_extended, length)
    split_at = n_heads * HEAD_DIM
    x_conv = active[:split_at]
    b_conv = active[split_at : split_at + STATE]
    c_conv = active[split_at + STATE :]
    step_size = jax.nn.softplus(dt_pre + bias_dt[:, None])
    log_decay = step_size * (-jnp.exp(log_rate))[:, None]
    return span_terms(
        x_conv,
        b_conv,
        c_conv,
        step_size,
        log_decay,
        segment_extended[TAPS - 1 :],
        segment_extended[TAPS - 2],
        skip_gain,
    )


def conv_part(raw_chan, rim_chan, weight, bias, segment_extended):
    padded = jnp.concatenate([rim_chan, raw_chan], axis=1)
    return conv_silu(padded, weight, bias, segment_extended, raw_chan.shape[1])


def scan_part(x_conv, b_conv, c_conv, dt_pre, bias_dt, log_rate, skip_gain, segment_extended):
    step_size = jax.nn.softplus(dt_pre + bias_dt[:, None])
    log_decay = step_size * (-jnp.exp(log_rate))[:, None]
    return span_terms(
        x_conv,
        b_conv,
        c_conv,
        step_size,
        log_decay,
        segment_extended[TAPS - 1 :],
        segment_extended[TAPS - 2],
        skip_gain,
    )


def weighted_sum(weight, stacked):
    return jnp.sum(weight[..., None, None] * stacked, axis=-3)


def span_fold(carry, states, state_start):
    blocks = carry.shape[-1]
    idx = jnp.arange(blocks)
    inside = (idx[None, :, None] < idx[None, None, :]) & (idx[None, None, :] < idx[:, None, None])
    link = jnp.prod(jnp.where(inside[None], carry[:, None, None, :], 1.0), axis=-1)
    link = link * (idx[None, :] < idx[:, None]).astype(jnp.float32)[None]
    lead = jnp.prod(jnp.where((idx[None, :] < idx[:, None])[None], carry[:, None, :], 1.0), axis=-1)
    tail = jnp.prod(jnp.where((idx[None, :] > idx[:, None])[None], carry[:, None, :], 1.0), axis=-1)
    starts = weighted_sum(link, states[:, None]) + lead[..., None, None] * state_start[:, None]
    state_end = weighted_sum(tail, states) + jnp.prod(carry, axis=-1)[:, None, None] * state_start
    return (jnp.moveaxis(starts, 1, 0), state_end)


def assemble(y_intra, c_three, entry, carry, states, state_start):
    starts, state_end = span_fold(carry, states, state_start)
    y_full = y_intra + jnp.einsum("nci,hci,chpn->hpci", c_three, entry, starts, precision=precise)
    return (y_full.reshape(y_full.shape[0] * y_full.shape[1], -1), state_end)


def reach(carry):

    def reach_advance(product, factor):
        return (product * factor, product)

    total, before = lax.scan(
        reach_advance, jnp.ones(carry.shape[:-1], jnp.float32), jnp.moveaxis(carry, -1, 0)
    )
    return (jnp.moveaxis(before, 0, -1), total)


def shards(
    x_in, b_in, c_in, dt_raw, cotangent, conv_weight, conv_bias, dt_bias, a_log, d_skip, doc_lengths
):
    lane = lax.axis_index("seq")
    x_width = x_in.shape[1]
    n_heads = dt_raw.shape[1]
    length = x_in.shape[2]
    blocks = length // SPAN
    groups_held = conv_weight.shape[0]
    packed = jnp.concatenate(
        [
            conv_weight.reshape(groups_held, -1),
            conv_bias,
            dt_bias,
            a_log,
            d_skip,
        ],
        axis=1,
    )
    slots = jnp.zeros((lax.axis_size("head") * groups_held, packed.shape[1]), packed.dtype)
    slots = lax.dynamic_update_slice_in_dim(slots, packed, lax.axis_index("head") * groups_held, 0)
    packed_all = lax.psum(slots, "head")
    cuts = [conv_weight[0].size, conv_bias.shape[1], dt_bias.shape[1], a_log.shape[1]]
    bounds = [sum(cuts[:k]) for k in range(len(cuts) + 1)]
    weight_all = packed_all[:, : bounds[1]].reshape((-1,) + conv_weight.shape[1:])
    bias_all = packed_all[:, bounds[1] : bounds[2]]
    dt_bias_all = packed_all[:, bounds[2] : bounds[3]]
    a_log_all = packed_all[:, bounds[3] : bounds[4]]
    d_skip_all = packed_all[:, bounds[4] :]
    x_total = weight_all.shape[2] - 2 * STATE

    b_width = b_in.shape[1]

    def own_channels(table):
        pieces = [
            lax.dynamic_slice_in_dim(table, start + lane * width, width, axis=table.ndim - 1)
            for start, width in ((0, x_width), (x_total, b_width), (x_total + STATE, b_width))
        ]
        return (pieces[0], jnp.concatenate(pieces[1:], axis=table.ndim - 1))

    weight_x, weight_bc = own_channels(weight_all)
    bias_x, bias_bc = own_channels(bias_all)
    dt_bias_here = lax.dynamic_slice_in_dim(dt_bias_all, lane * n_heads, n_heads, axis=1)
    a_log_here = lax.dynamic_slice_in_dim(a_log_all, lane * n_heads, n_heads, axis=1)
    d_skip_here = lax.dynamic_slice_in_dim(d_skip_all, lane * n_heads, n_heads, axis=1)
    groups_here = x_in.shape[0]
    raw_chan = jnp.concatenate([x_in, b_in, c_in], axis=1)
    rim_chan = passed_along(raw_chan[:, :, length - (TAPS - 1) :], "head", 1)
    rank = lax.axis_index("head")
    positions = rank * length + jnp.arange(-(TAPS - 1), length, dtype=jnp.int32)
    segment_extended = segment_ids(positions, doc_lengths)
    each_group = (0, 0, 0, 0, None)

    def own_conv(x_float, bc_float, rim_float):
        x_conv = jax.vmap(conv_part, in_axes=each_group)(
            x_float, rim_float[:, :x_width], weight_x, bias_x, segment_extended
        )
        bc_conv = jax.vmap(conv_part, in_axes=each_group)(
            bc_float, rim_float[:, x_width:], weight_bc, bias_bc, segment_extended
        )
        return (x_conv, bc_conv)

    (x_conv, bc_conv), pull_conv = jax.vjp(
        own_conv,
        x_in.astype(jnp.float32),
        jnp.concatenate([b_in, c_in], axis=1).astype(jnp.float32),
        rim_chan.astype(jnp.float32),
    )
    b_conv = lax.all_gather(bc_conv[:, :b_width], "seq", axis=1, tiled=True)
    c_conv = lax.all_gather(bc_conv[:, b_width:], "seq", axis=1, tiled=True)

    def local_terms(x_float, b_float, c_float, dt_float):
        return jax.vmap(scan_part, in_axes=(0, 0, 0, 0, 0, 0, 0, None))(
            x_float,
            b_float,
            c_float,
            dt_float,
            dt_bias_here,
            a_log_here,
            d_skip_here,
            segment_extended,
        )

    terms, pull_terms = jax.vjp(local_terms, x_conv, b_conv, c_conv, dt_raw.astype(jnp.float32))
    y_intra, c_three, entry, carry, states = terms
    before, total = reach(carry)
    state_zero = jnp.zeros((groups_here, n_heads, HEAD_DIM, STATE), jnp.float32)
    _, summary = jax.vmap(span_fold)(carry, states, state_zero)
    cot_float = cotangent.astype(jnp.float32)
    cot_five = cot_float.reshape(groups_here, n_heads, HEAD_DIM, blocks, SPAN)
    local_grad = jnp.einsum(
        "ghpci,ghci,gnci->ghpn", cot_five, entry * before[..., None], c_three, precision=precise
    )
    state_in, grad_out = carried_both(total, summary, local_grad, "head")

    def finish(pieces, state_start):
        return jax.vmap(assemble)(
            pieces[0], pieces[1], pieces[2], pieces[3], pieces[4], state_start
        )

    (y_scan, state_out), pull_out = jax.vjp(finish, terms, state_in)
    y_out = y_scan.astype(jnp.bfloat16)
    d_terms, _ = pull_out((cot_float, grad_out))
    d_x_conv, d_b_conv, d_c_conv, d_dt = pull_terms(d_terms)
    d_bc_conv = jnp.concatenate(
        [
            lax.psum_scatter(d_b_conv, "seq", scatter_dimension=1, tiled=True),
            lax.psum_scatter(d_c_conv, "seq", scatter_dimension=1, tiled=True),
        ],
        axis=1,
    )
    d_x, d_bc, d_rim = pull_conv((d_x_conv, d_bc_conv))
    d_raw = jnp.concatenate([d_x, d_bc], axis=1)
    returned = passed_along(d_rim, "head", -1)
    cut_at = length - (TAPS - 1)
    d_raw = jnp.concatenate([d_raw[:, :, :cut_at], d_raw[:, :, cut_at:] + returned], axis=2)
    x_grad = d_raw[:, :x_width].astype(jnp.bfloat16)
    b_grad = d_raw[:, x_width : x_width + b_width].astype(jnp.bfloat16)
    c_grad = d_raw[:, x_width + b_width :].astype(jnp.bfloat16)
    dt_grad = d_dt.astype(jnp.bfloat16)
    return (y_out, x_grad, b_grad, c_grad, dt_grad)


def solution(mesh):
    return jax.shard_map(
        shards,
        mesh=mesh,
        in_specs=(
            P(None, "seq", "head"),
            P(None, "seq", "head"),
            P(None, "seq", "head"),
            P(None, "seq", "head"),
            P(None, "seq", "head"),
            P("head", None, None),
            P("head", None),
            P("head", None),
            P("head", None),
            P("head", None),
            P(),
        ),
        out_specs=(
            P(None, "seq", "head"),
            P(None, "seq", "head"),
            P(None, "seq", "head"),
            P(None, "seq", "head"),
            P(None, "seq", "head"),
        ),
        check_vma=False,
    )
```

```python
import jax
import jax.numpy as jnp
from jax import lax
from jax.sharding import PartitionSpec as P

HEAD_DIM = 64
STATE = 256
TAPS = 4
SPAN = 128


precise = lax.Precision.HIGHEST


def passed_along(value, axis, steps):
    count = lax.axis_size(axis)
    first, last = (max(0, -steps), min(count, count - steps))
    return lax.ppermute(value, axis, [(source, source + steps) for source in range(first, last)])


def carried_both(totals, ahead, behind, axis, beside):
    factor = totals[..., None, None]
    pair = lax.optimization_barrier((ahead, behind))
    received, beside = lax.optimization_barrier(
        ((passed_along(pair[0], axis, 1), passed_along(pair[1], axis, -1)), beside)
    )
    for _ in range(lax.axis_size(axis) - 2):
        received = lax.optimization_barrier(
            (
                passed_along(factor * received[0] + ahead, axis, 1),
                passed_along(factor * received[1] + behind, axis, -1),
            )
        )
    return received + (beside,)


def segment_ids(positions, doc_lengths):
    ends = jnp.cumsum(doc_lengths)
    counted = jnp.sum((ends[None, :] <= positions[:, None]).astype(jnp.int32), axis=1)
    return jnp.where(positions >= 0, counted, -1)


def conv_silu(padded, weight, bias, segment_extended, length):
    total = jnp.zeros((padded.shape[0], length), jnp.float32) + bias[:, None]
    for offset in range(TAPS):
        same_doc = (
            segment_extended[offset : offset + length] == segment_extended[TAPS - 1 :]
        ).astype(jnp.float32)
        total = (
            total
            + weight[offset][:, None] * padded[:, offset : offset + length] * same_doc[None, :]
        )
    return jax.nn.silu(total)


def span_terms(x_conv, b_conv, c_conv, step_size, log_decay, seg_tok, seg_before, skip_gain):
    n_heads, length = step_size.shape
    blocks = length // SPAN
    x_four = x_conv.reshape(n_heads, HEAD_DIM, blocks, SPAN)
    b_three = b_conv.reshape(STATE, blocks, SPAN)
    c_three = c_conv.reshape(STATE, blocks, SPAN)
    step_three = step_size.reshape(n_heads, blocks, SPAN)
    seg_two = seg_tok.reshape(blocks, SPAN)
    rows_idx = lax.broadcasted_iota(jnp.int32, (SPAN, SPAN), 0)
    cols_idx = lax.broadcasted_iota(jnp.int32, (SPAN, SPAN), 1)
    lower = (rows_idx >= cols_idx).astype(jnp.float32)
    cumul = jnp.einsum(
        "hcj,ij->hci", log_decay.reshape(n_heads, blocks, SPAN), lower, precision=precise
    )
    mask_doc = lower[None] * (seg_two[:, :, None] == seg_two[:, None, :]).astype(jnp.float32)
    decay = jnp.exp(jnp.minimum(cumul[:, :, :, None] - cumul[:, :, None, :], 0.0)) * mask_doc[None]
    scores = jnp.einsum("nci,ncj->cij", c_three, b_three, precision=precise)
    weighted = x_four * step_three[:, None]
    y_intra = jnp.einsum("hcij,hpcj->hpci", decay * scores[None], weighted, precision=precise)
    y_intra = y_intra + skip_gain[:, None, None, None] * x_four
    last_cum = cumul[:, :, -1:]
    keep_end = jnp.exp(last_cum - cumul) * (seg_two == seg_two[:, -1:]).astype(jnp.float32)[None]
    states = jnp.einsum("hpcj,hcj,ncj->hcpn", weighted, keep_end, b_three, precision=precise)
    prev_seg = jnp.concatenate([seg_before[None], seg_two[:-1, -1]])
    entry = jnp.exp(cumul) * (seg_two == prev_seg[:, None]).astype(jnp.float32)[None]
    carry = jnp.exp(last_cum[:, :, 0]) * (seg_two[:, -1] == prev_seg).astype(jnp.float32)[None]
    return (y_intra, c_three, entry, carry, states)


def group_terms(
    raw_chan, rim_chan, dt_pre, weight, bias, bias_dt, log_rate, skip_gain, segment_extended
):
    n_heads = dt_pre.shape[0]
    length = raw_chan.shape[1]
    padded = jnp.concatenate([rim_chan, raw_chan], axis=1)
    active = conv_silu(padded, weight, bias, segment_extended, length)
    split_at = n_heads * HEAD_DIM
    x_conv = active[:split_at]
    b_conv = active[split_at : split_at + STATE]
    c_conv = active[split_at + STATE :]
    step_size = jax.nn.softplus(dt_pre + bias_dt[:, None])
    log_decay = step_size * (-jnp.exp(log_rate))[:, None]
    return span_terms(
        x_conv,
        b_conv,
        c_conv,
        step_size,
        log_decay,
        segment_extended[TAPS - 1 :],
        segment_extended[TAPS - 2],
        skip_gain,
    )


def conv_part(raw_chan, rim_chan, weight, bias, segment_extended):
    padded = jnp.concatenate([rim_chan, raw_chan], axis=1)
    return conv_silu(padded, weight, bias, segment_extended, raw_chan.shape[1])


def scan_part(x_conv, b_conv, c_conv, dt_pre, bias_dt, log_rate, skip_gain, segment_extended):
    step_size = jax.nn.softplus(dt_pre + bias_dt[:, None])
    log_decay = step_size * (-jnp.exp(log_rate))[:, None]
    return span_terms(
        x_conv,
        b_conv,
        c_conv,
        step_size,
        log_decay,
        segment_extended[TAPS - 1 :],
        segment_extended[TAPS - 2],
        skip_gain,
    )


def weighted_sum(weight, stacked):
    return jnp.sum(weight[..., None, None] * stacked, axis=-3)


def span_fold(carry, states, state_start):
    blocks = carry.shape[-1]
    idx = jnp.arange(blocks)
    inside = (idx[None, :, None] < idx[None, None, :]) & (idx[None, None, :] < idx[:, None, None])
    link = jnp.prod(jnp.where(inside[None], carry[:, None, None, :], 1.0), axis=-1)
    link = link * (idx[None, :] < idx[:, None]).astype(jnp.float32)[None]
    lead = jnp.prod(jnp.where((idx[None, :] < idx[:, None])[None], carry[:, None, :], 1.0), axis=-1)
    tail = jnp.prod(jnp.where((idx[None, :] > idx[:, None])[None], carry[:, None, :], 1.0), axis=-1)
    starts = weighted_sum(link, states[:, None]) + lead[..., None, None] * state_start[:, None]
    state_end = weighted_sum(tail, states) + jnp.prod(carry, axis=-1)[:, None, None] * state_start
    return (jnp.moveaxis(starts, 1, 0), state_end)


def assemble(y_intra, c_three, entry, carry, states, state_start):
    starts, state_end = span_fold(carry, states, state_start)
    y_full = y_intra + jnp.einsum("nci,hci,chpn->hpci", c_three, entry, starts, precision=precise)
    return (y_full.reshape(y_full.shape[0] * y_full.shape[1], -1), state_end)


def reach(carry):

    def reach_advance(product, factor):
        return (product * factor, product)

    total, before = lax.scan(
        reach_advance, jnp.ones(carry.shape[:-1], jnp.float32), jnp.moveaxis(carry, -1, 0)
    )
    return (jnp.moveaxis(before, 0, -1), total)


def shards(
    x_in, b_in, c_in, dt_raw, cotangent, conv_weight, conv_bias, dt_bias, a_log, d_skip, doc_lengths
):
    lane = lax.axis_index("seq")
    x_width = x_in.shape[1]
    n_heads = dt_raw.shape[1]
    length = x_in.shape[2]
    blocks = length // SPAN
    groups_held = conv_weight.shape[0]
    packed = jnp.concatenate(
        [
            conv_weight.reshape(groups_held, -1),
            conv_bias,
            dt_bias,
            a_log,
            d_skip,
        ],
        axis=1,
    )
    packed_all = lax.all_gather(packed, "head", axis=0, tiled=True)
    cuts = [conv_weight[0].size, conv_bias.shape[1], dt_bias.shape[1], a_log.shape[1]]
    bounds = [sum(cuts[:k]) for k in range(len(cuts) + 1)]
    weight_all = packed_all[:, : bounds[1]].reshape((-1,) + conv_weight.shape[1:])
    bias_all = packed_all[:, bounds[1] : bounds[2]]
    dt_bias_all = packed_all[:, bounds[2] : bounds[3]]
    a_log_all = packed_all[:, bounds[3] : bounds[4]]
    d_skip_all = packed_all[:, bounds[4] :]
    x_total = weight_all.shape[2] - 2 * STATE

    b_width = b_in.shape[1]

    def own_channels(table):
        pieces = [
            lax.dynamic_slice_in_dim(table, start + lane * width, width, axis=table.ndim - 1)
            for start, width in ((0, x_width), (x_total, b_width), (x_total + STATE, b_width))
        ]
        return (pieces[0], jnp.concatenate(pieces[1:], axis=table.ndim - 1))

    weight_x, weight_bc = own_channels(weight_all)
    bias_x, bias_bc = own_channels(bias_all)
    dt_bias_here = lax.dynamic_slice_in_dim(dt_bias_all, lane * n_heads, n_heads, axis=1)
    a_log_here = lax.dynamic_slice_in_dim(a_log_all, lane * n_heads, n_heads, axis=1)
    d_skip_here = lax.dynamic_slice_in_dim(d_skip_all, lane * n_heads, n_heads, axis=1)
    groups_here = x_in.shape[0]
    raw_chan = jnp.concatenate([x_in, b_in, c_in], axis=1)
    rim_chan = passed_along(raw_chan[:, :, length - (TAPS - 1) :], "head", 1)
    rank = lax.axis_index("head")
    positions = rank * length + jnp.arange(-(TAPS - 1), length, dtype=jnp.int32)
    segment_extended = segment_ids(positions, doc_lengths)
    each_group = (0, 0, 0, 0, None)

    def own_conv(x_float, bc_float, rim_float):
        x_conv = jax.vmap(conv_part, in_axes=each_group)(
            x_float, rim_float[:, :x_width], weight_x, bias_x, segment_extended
        )
        bc_conv = jax.vmap(conv_part, in_axes=each_group)(
            bc_float, rim_float[:, x_width:], weight_bc, bias_bc, segment_extended
        )
        return (x_conv, bc_conv)

    (x_conv, bc_conv), pull_conv = jax.vjp(
        own_conv,
        x_in.astype(jnp.float32),
        jnp.concatenate([b_in, c_in], axis=1).astype(jnp.float32),
        rim_chan.astype(jnp.float32),
    )
    b_conv = lax.all_gather(bc_conv[:, :b_width], "seq", axis=1, tiled=True)
    c_conv = lax.all_gather(bc_conv[:, b_width:], "seq", axis=1, tiled=True)

    def local_terms(x_float, b_float, c_float, dt_float):
        return jax.vmap(scan_part, in_axes=(0, 0, 0, 0, 0, 0, 0, None))(
            x_float,
            b_float,
            c_float,
            dt_float,
            dt_bias_here,
            a_log_here,
            d_skip_here,
            segment_extended,
        )

    operands = (x_conv, b_conv, c_conv, dt_raw.astype(jnp.float32))
    y_intra, pull_intra = jax.vjp(lambda *a: local_terms(*a)[0], *operands)
    cross, pull_cross = jax.vjp(lambda *a: local_terms(*a)[1:], *operands)
    terms = (y_intra,) + tuple(cross)
    c_three, entry, carry, states = cross
    before, total = reach(carry)
    state_zero = jnp.zeros((groups_here, n_heads, HEAD_DIM, STATE), jnp.float32)
    _, summary = jax.vmap(span_fold)(carry, states, state_zero)
    cot_float = cotangent.astype(jnp.float32)
    cot_five = cot_float.reshape(groups_here, n_heads, HEAD_DIM, blocks, SPAN)
    local_grad = jnp.einsum(
        "ghpci,ghci,gnci->ghpn", cot_five, entry * before[..., None], c_three, precision=precise
    )
    d_intra = pull_intra(cot_float.reshape(y_intra.shape))
    state_in, grad_out, d_intra = carried_both(total, summary, local_grad, "head", d_intra)

    def finish(pieces, state_start):
        return jax.vmap(assemble)(
            pieces[0], pieces[1], pieces[2], pieces[3], pieces[4], state_start
        )

    (y_scan, state_out), pull_out = jax.vjp(finish, terms, state_in)
    y_out = y_scan.astype(jnp.bfloat16)
    d_terms, _ = pull_out((cot_float, grad_out))
    d_x_conv, d_b_conv, d_c_conv, d_dt = (
        a + b for a, b in zip(pull_cross(tuple(d_terms[1:])), d_intra)
    )
    d_bc_conv = jnp.concatenate(
        [
            lax.psum_scatter(d_b_conv, "seq", scatter_dimension=1, tiled=True),
            lax.psum_scatter(d_c_conv, "seq", scatter_dimension=1, tiled=True),
        ],
        axis=1,
    )
    d_x, d_bc, d_rim = pull_conv((d_x_conv, d_bc_conv))
    d_raw = jnp.concatenate([d_x, d_bc], axis=1)
    returned = passed_along(d_rim, "head", -1)
    cut_at = length - (TAPS - 1)
    d_raw = jnp.concatenate([d_raw[:, :, :cut_at], d_raw[:, :, cut_at:] + returned], axis=2)
    x_grad = d_raw[:, :x_width].astype(jnp.bfloat16)
    b_grad = d_raw[:, x_width : x_width + b_width].astype(jnp.bfloat16)
    c_grad = d_raw[:, x_width + b_width :].astype(jnp.bfloat16)
    dt_grad = d_dt.astype(jnp.bfloat16)
    return (y_out, x_grad, b_grad, c_grad, dt_grad)


def solution(mesh):
    return jax.shard_map(
        shards,
        mesh=mesh,
        in_specs=(
            P(None, "seq", "head"),
            P(None, "seq", "head"),
            P(None, "seq", "head"),
            P(None, "seq", "head"),
            P(None, "seq", "head"),
            P("head", None, None),
            P("head", None),
            P("head", None),
            P("head", None),
            P("head", None),
            P(),
        ),
        out_specs=(
            P(None, "seq", "head"),
            P(None, "seq", "head"),
            P(None, "seq", "head"),
            P(None, "seq", "head"),
            P(None, "seq", "head"),
        ),
        check_vma=False,
    )
```

```python
import jax
import jax.numpy as jnp
from jax import lax
from jax.sharding import PartitionSpec as P

HEAD_DIM = 64
STATE = 256
TAPS = 4
SPAN = 128


precise = lax.Precision.HIGHEST


def passed_along(value, axis, steps):
    count = lax.axis_size(axis)
    first, last = (max(0, -steps), min(count, count - steps))
    return lax.ppermute(value, axis, [(source, source + steps) for source in range(first, last)])


def carried_both(totals, ahead, behind, axis):
    factor = totals[..., None, None]
    pair = lax.optimization_barrier((ahead, behind))
    received = lax.optimization_barrier(
        (passed_along(pair[0], axis, 1), passed_along(pair[1], axis, -1))
    )
    for _ in range(lax.axis_size(axis) - 2):
        received = lax.optimization_barrier(
            (
                passed_along(factor * received[0] + ahead, axis, 1),
                passed_along(factor * received[1] + behind, axis, -1),
            )
        )
    return received


def segment_ids(positions, doc_lengths):
    ends = jnp.cumsum(doc_lengths)
    counted = jnp.sum((ends[None, :] <= positions[:, None]).astype(jnp.int32), axis=1)
    return jnp.where(positions >= 0, counted, -1)


def conv_silu(padded, weight, bias, segment_extended, length):
    total = jnp.zeros((padded.shape[0], length), jnp.float32) + bias[:, None]
    for offset in range(TAPS):
        same_doc = (
            segment_extended[offset : offset + length] == segment_extended[TAPS - 1 :]
        ).astype(jnp.float32)
        total = (
            total
            + weight[offset][:, None] * padded[:, offset : offset + length] * same_doc[None, :]
        )
    return jax.nn.silu(total)


def span_terms(x_conv, b_conv, c_conv, step_size, log_decay, seg_tok, seg_before, skip_gain):
    n_heads, length = step_size.shape
    blocks = length // SPAN
    x_four = x_conv.reshape(n_heads, HEAD_DIM, blocks, SPAN)
    b_three = b_conv.reshape(STATE, blocks, SPAN)
    c_three = c_conv.reshape(STATE, blocks, SPAN)
    step_three = step_size.reshape(n_heads, blocks, SPAN)
    seg_two = seg_tok.reshape(blocks, SPAN)
    rows_idx = lax.broadcasted_iota(jnp.int32, (SPAN, SPAN), 0)
    cols_idx = lax.broadcasted_iota(jnp.int32, (SPAN, SPAN), 1)
    lower = (rows_idx >= cols_idx).astype(jnp.float32)
    cumul = jnp.einsum(
        "hcj,ij->hci", log_decay.reshape(n_heads, blocks, SPAN), lower, precision=precise
    )
    mask_doc = lower[None] * (seg_two[:, :, None] == seg_two[:, None, :]).astype(jnp.float32)
    decay = jnp.exp(jnp.minimum(cumul[:, :, :, None] - cumul[:, :, None, :], 0.0)) * mask_doc[None]
    scores = jnp.einsum("nci,ncj->cij", c_three, b_three, precision=precise)
    weighted = x_four * step_three[:, None]
    y_intra = jnp.einsum("hcij,hpcj->hpci", decay * scores[None], weighted, precision=precise)
    y_intra = y_intra + skip_gain[:, None, None, None] * x_four
    last_cum = cumul[:, :, -1:]
    keep_end = jnp.exp(last_cum - cumul) * (seg_two == seg_two[:, -1:]).astype(jnp.float32)[None]
    states = jnp.einsum("hpcj,hcj,ncj->hcpn", weighted, keep_end, b_three, precision=precise)
    prev_seg = jnp.concatenate([seg_before[None], seg_two[:-1, -1]])
    entry = jnp.exp(cumul) * (seg_two == prev_seg[:, None]).astype(jnp.float32)[None]
    carry = jnp.exp(last_cum[:, :, 0]) * (seg_two[:, -1] == prev_seg).astype(jnp.float32)[None]
    return (y_intra, c_three, entry, carry, states)


def group_terms(
    raw_chan, rim_chan, dt_pre, weight, bias, bias_dt, log_rate, skip_gain, segment_extended
):
    n_heads = dt_pre.shape[0]
    length = raw_chan.shape[1]
    padded = jnp.concatenate([rim_chan, raw_chan], axis=1)
    active = conv_silu(padded, weight, bias, segment_extended, length)
    split_at = n_heads * HEAD_DIM
    x_conv = active[:split_at]
    b_conv = active[split_at : split_at + STATE]
    c_conv = active[split_at + STATE :]
    step_size = jax.nn.softplus(dt_pre + bias_dt[:, None])
    log_decay = step_size * (-jnp.exp(log_rate))[:, None]
    return span_terms(
        x_conv,
        b_conv,
        c_conv,
        step_size,
        log_decay,
        segment_extended[TAPS - 1 :],
        segment_extended[TAPS - 2],
        skip_gain,
    )


def conv_part(raw_chan, rim_chan, weight, bias, segment_extended):
    padded = jnp.concatenate([rim_chan, raw_chan], axis=1)
    return conv_silu(padded, weight, bias, segment_extended, raw_chan.shape[1])


def scan_part(x_conv, b_conv, c_conv, dt_pre, bias_dt, log_rate, skip_gain, segment_extended):
    step_size = jax.nn.softplus(dt_pre + bias_dt[:, None])
    log_decay = step_size * (-jnp.exp(log_rate))[:, None]
    return span_terms(
        x_conv,
        b_conv,
        c_conv,
        step_size,
        log_decay,
        segment_extended[TAPS - 1 :],
        segment_extended[TAPS - 2],
        skip_gain,
    )


def weighted_sum(weight, stacked):
    return jnp.sum(weight[..., None, None] * stacked, axis=-3)


def span_fold(carry, states, state_start):
    blocks = carry.shape[-1]
    idx = jnp.arange(blocks)
    inside = (idx[None, :, None] < idx[None, None, :]) & (idx[None, None, :] < idx[:, None, None])
    link = jnp.prod(jnp.where(inside[None], carry[:, None, None, :], 1.0), axis=-1)
    link = link * (idx[None, :] < idx[:, None]).astype(jnp.float32)[None]
    lead = jnp.prod(jnp.where((idx[None, :] < idx[:, None])[None], carry[:, None, :], 1.0), axis=-1)
    tail = jnp.prod(jnp.where((idx[None, :] > idx[:, None])[None], carry[:, None, :], 1.0), axis=-1)
    starts = weighted_sum(link, states[:, None]) + lead[..., None, None] * state_start[:, None]
    state_end = weighted_sum(tail, states) + jnp.prod(carry, axis=-1)[:, None, None] * state_start
    return (jnp.moveaxis(starts, 1, 0), state_end)


def assemble(y_intra, c_three, entry, carry, states, state_start):
    starts, state_end = span_fold(carry, states, state_start)
    y_full = y_intra + jnp.einsum("nci,hci,chpn->hpci", c_three, entry, starts, precision=precise)
    return (y_full.reshape(y_full.shape[0] * y_full.shape[1], -1), state_end)


def reach(carry):

    def reach_advance(product, factor):
        return (product * factor, product)

    total, before = lax.scan(
        reach_advance, jnp.ones(carry.shape[:-1], jnp.float32), jnp.moveaxis(carry, -1, 0)
    )
    return (jnp.moveaxis(before, 0, -1), total)


def shards(
    x_in, b_in, c_in, dt_raw, cotangent, conv_weight, conv_bias, dt_bias, a_log, d_skip, doc_lengths
):
    lane = lax.axis_index("seq")
    x_width = x_in.shape[1]
    n_heads = dt_raw.shape[1]
    length = x_in.shape[2]
    blocks = length // SPAN
    groups_held = conv_weight.shape[0]
    packed = jnp.concatenate(
        [
            conv_weight.reshape(groups_held, -1),
            conv_bias,
            dt_bias,
            a_log,
            d_skip,
        ],
        axis=1,
    )
    count, here = (lax.axis_size("head"), lax.axis_index("head"))
    stacked = jnp.stack(
        [packed]
        + [
            lax.ppermute(packed, "head", [(i, (i + k) % count) for i in range(count)])
            for k in range(1, count)
        ]
    )
    order = (here - jnp.arange(count)) % count
    packed_all = jnp.take(stacked, order, axis=0).reshape((-1, packed.shape[1]))
    cuts = [conv_weight[0].size, conv_bias.shape[1], dt_bias.shape[1], a_log.shape[1]]
    bounds = [sum(cuts[:k]) for k in range(len(cuts) + 1)]
    weight_all = packed_all[:, : bounds[1]].reshape((-1,) + conv_weight.shape[1:])
    bias_all = packed_all[:, bounds[1] : bounds[2]]
    dt_bias_all = packed_all[:, bounds[2] : bounds[3]]
    a_log_all = packed_all[:, bounds[3] : bounds[4]]
    d_skip_all = packed_all[:, bounds[4] :]
    x_total = weight_all.shape[2] - 2 * STATE

    b_width = b_in.shape[1]

    def own_channels(table):
        pieces = [
            lax.dynamic_slice_in_dim(table, start + lane * width, width, axis=table.ndim - 1)
            for start, width in ((0, x_width), (x_total, b_width), (x_total + STATE, b_width))
        ]
        return (pieces[0], jnp.concatenate(pieces[1:], axis=table.ndim - 1))

    weight_x, weight_bc = own_channels(weight_all)
    bias_x, bias_bc = own_channels(bias_all)
    dt_bias_here = lax.dynamic_slice_in_dim(dt_bias_all, lane * n_heads, n_heads, axis=1)
    a_log_here = lax.dynamic_slice_in_dim(a_log_all, lane * n_heads, n_heads, axis=1)
    d_skip_here = lax.dynamic_slice_in_dim(d_skip_all, lane * n_heads, n_heads, axis=1)
    groups_here = x_in.shape[0]
    raw_chan = jnp.concatenate([x_in, b_in, c_in], axis=1)
    rim_chan = passed_along(raw_chan[:, :, length - (TAPS - 1) :], "head", 1)
    rank = lax.axis_index("head")
    positions = rank * length + jnp.arange(-(TAPS - 1), length, dtype=jnp.int32)
    segment_extended = segment_ids(positions, doc_lengths)
    each_group = (0, 0, 0, 0, None)

    def own_conv(x_float, bc_float, rim_float):
        x_conv = jax.vmap(conv_part, in_axes=each_group)(
            x_float, rim_float[:, :x_width], weight_x, bias_x, segment_extended
        )
        bc_conv = jax.vmap(conv_part, in_axes=each_group)(
            bc_float, rim_float[:, x_width:], weight_bc, bias_bc, segment_extended
        )
        return (x_conv, bc_conv)

    (x_conv, bc_conv), pull_conv = jax.vjp(
        own_conv,
        x_in.astype(jnp.float32),
        jnp.concatenate([b_in, c_in], axis=1).astype(jnp.float32),
        rim_chan.astype(jnp.float32),
    )
    b_conv = lax.all_gather(bc_conv[:, :b_width], "seq", axis=1, tiled=True)
    c_conv = lax.all_gather(bc_conv[:, b_width:], "seq", axis=1, tiled=True)

    def local_terms(x_float, b_float, c_float, dt_float):
        return jax.vmap(scan_part, in_axes=(0, 0, 0, 0, 0, 0, 0, None))(
            x_float,
            b_float,
            c_float,
            dt_float,
            dt_bias_here,
            a_log_here,
            d_skip_here,
            segment_extended,
        )

    terms, pull_terms = jax.vjp(local_terms, x_conv, b_conv, c_conv, dt_raw.astype(jnp.float32))
    y_intra, c_three, entry, carry, states = terms
    before, total = reach(carry)
    state_zero = jnp.zeros((groups_here, n_heads, HEAD_DIM, STATE), jnp.float32)
    _, summary = jax.vmap(span_fold)(carry, states, state_zero)
    cot_float = cotangent.astype(jnp.float32)
    cot_five = cot_float.reshape(groups_here, n_heads, HEAD_DIM, blocks, SPAN)
    local_grad = jnp.einsum(
        "ghpci,ghci,gnci->ghpn", cot_five, entry * before[..., None], c_three, precision=precise
    )
    state_in, grad_out = carried_both(total, summary, local_grad, "head")

    def finish(pieces, state_start):
        return jax.vmap(assemble)(
            pieces[0], pieces[1], pieces[2], pieces[3], pieces[4], state_start
        )

    (y_scan, state_out), pull_out = jax.vjp(finish, terms, state_in)
    y_out = y_scan.astype(jnp.bfloat16)
    d_terms, _ = pull_out((cot_float, grad_out))
    d_x_conv, d_b_conv, d_c_conv, d_dt = pull_terms(d_terms)
    d_bc_conv = jnp.concatenate(
        [
            lax.psum_scatter(d_b_conv, "seq", scatter_dimension=1, tiled=True),
            lax.psum_scatter(d_c_conv, "seq", scatter_dimension=1, tiled=True),
        ],
        axis=1,
    )
    d_x, d_bc, d_rim = pull_conv((d_x_conv, d_bc_conv))
    d_raw = jnp.concatenate([d_x, d_bc], axis=1)
    returned = passed_along(d_rim, "head", -1)
    cut_at = length - (TAPS - 1)
    d_raw = jnp.concatenate([d_raw[:, :, :cut_at], d_raw[:, :, cut_at:] + returned], axis=2)
    x_grad = d_raw[:, :x_width].astype(jnp.bfloat16)
    b_grad = d_raw[:, x_width : x_width + b_width].astype(jnp.bfloat16)
    c_grad = d_raw[:, x_width + b_width :].astype(jnp.bfloat16)
    dt_grad = d_dt.astype(jnp.bfloat16)
    return (y_out, x_grad, b_grad, c_grad, dt_grad)


def solution(mesh):
    return jax.shard_map(
        shards,
        mesh=mesh,
        in_specs=(
            P(None, "seq", "head"),
            P(None, "seq", "head"),
            P(None, "seq", "head"),
            P(None, "seq", "head"),
            P(None, "seq", "head"),
            P("head", None, None),
            P("head", None),
            P("head", None),
            P("head", None),
            P("head", None),
            P(),
        ),
        out_specs=(
            P(None, "seq", "head"),
            P(None, "seq", "head"),
            P(None, "seq", "head"),
            P(None, "seq", "head"),
            P(None, "seq", "head"),
        ),
        check_vma=False,
    )
```

```python
import jax
import jax.numpy as jnp
from jax import lax
from jax.sharding import PartitionSpec as P

HEAD_DIM = 64
STATE = 256
TAPS = 4
SPAN = 128


precise = lax.Precision.HIGHEST


def passed_along(value, axis, steps):
    count = lax.axis_size(axis)
    first, last = (max(0, -steps), min(count, count - steps))
    return lax.ppermute(value, axis, [(source, source + steps) for source in range(first, last)])


def carried_both(totals, ahead, behind, axis):
    factor = totals[..., None, None]
    pair = lax.optimization_barrier((ahead, behind))
    received = lax.optimization_barrier(
        (passed_along(pair[0], axis, 1), passed_along(pair[1], axis, -1))
    )
    for _ in range(lax.axis_size(axis) - 2):
        received = lax.optimization_barrier(
            (
                passed_along(factor * received[0] + ahead, axis, 1),
                passed_along(factor * received[1] + behind, axis, -1),
            )
        )
    return received


def segment_ids(positions, doc_lengths):
    ends = jnp.cumsum(doc_lengths)
    counted = jnp.sum((ends[None, :] <= positions[:, None]).astype(jnp.int32), axis=1)
    return jnp.where(positions >= 0, counted, -1)


def conv_silu(padded, weight, bias, segment_extended, length):
    total = jnp.zeros((padded.shape[0], length), jnp.float32) + bias[:, None]
    for offset in range(TAPS):
        same_doc = (
            segment_extended[offset : offset + length] == segment_extended[TAPS - 1 :]
        ).astype(jnp.float32)
        total = (
            total
            + weight[offset][:, None] * padded[:, offset : offset + length] * same_doc[None, :]
        )
    return jax.nn.silu(total)


def span_terms(x_conv, b_conv, c_conv, step_size, log_decay, seg_tok, seg_before, skip_gain):
    n_heads, length = step_size.shape
    blocks = length // SPAN
    x_four = x_conv.reshape(n_heads, HEAD_DIM, blocks, SPAN)
    b_three = b_conv.reshape(STATE, blocks, SPAN)
    c_three = c_conv.reshape(STATE, blocks, SPAN)
    step_three = step_size.reshape(n_heads, blocks, SPAN)
    seg_two = seg_tok.reshape(blocks, SPAN)
    rows_idx = lax.broadcasted_iota(jnp.int32, (SPAN, SPAN), 0)
    cols_idx = lax.broadcasted_iota(jnp.int32, (SPAN, SPAN), 1)
    lower = (rows_idx >= cols_idx).astype(jnp.float32)
    cumul = jnp.einsum(
        "hcj,ij->hci", log_decay.reshape(n_heads, blocks, SPAN), lower, precision=precise
    )
    mask_doc = lower[None] * (seg_two[:, :, None] == seg_two[:, None, :]).astype(jnp.float32)
    decay = jnp.exp(jnp.minimum(cumul[:, :, :, None] - cumul[:, :, None, :], 0.0)) * mask_doc[None]
    scores = jnp.einsum("nci,ncj->cij", c_three, b_three, precision=precise)
    weighted = x_four * step_three[:, None]
    y_intra = jnp.einsum("hcij,hpcj->hpci", decay * scores[None], weighted, precision=precise)
    y_intra = y_intra + skip_gain[:, None, None, None] * x_four
    last_cum = cumul[:, :, -1:]
    keep_end = jnp.exp(last_cum - cumul) * (seg_two == seg_two[:, -1:]).astype(jnp.float32)[None]
    states = jnp.einsum("hpcj,hcj,ncj->hcpn", weighted, keep_end, b_three, precision=precise)
    prev_seg = jnp.concatenate([seg_before[None], seg_two[:-1, -1]])
    entry = jnp.exp(cumul) * (seg_two == prev_seg[:, None]).astype(jnp.float32)[None]
    carry = jnp.exp(last_cum[:, :, 0]) * (seg_two[:, -1] == prev_seg).astype(jnp.float32)[None]
    return (y_intra, c_three, entry, carry, states)


def group_terms(
    raw_chan, rim_chan, dt_pre, weight, bias, bias_dt, log_rate, skip_gain, segment_extended
):
    n_heads = dt_pre.shape[0]
    length = raw_chan.shape[1]
    padded = jnp.concatenate([rim_chan, raw_chan], axis=1)
    active = conv_silu(padded, weight, bias, segment_extended, length)
    split_at = n_heads * HEAD_DIM
    x_conv = active[:split_at]
    b_conv = active[split_at : split_at + STATE]
    c_conv = active[split_at + STATE :]
    step_size = jax.nn.softplus(dt_pre + bias_dt[:, None])
    log_decay = step_size * (-jnp.exp(log_rate))[:, None]
    return span_terms(
        x_conv,
        b_conv,
        c_conv,
        step_size,
        log_decay,
        segment_extended[TAPS - 1 :],
        segment_extended[TAPS - 2],
        skip_gain,
    )


def conv_part(raw_chan, rim_chan, weight, bias, segment_extended):
    padded = jnp.concatenate([rim_chan, raw_chan], axis=1)
    return conv_silu(padded, weight, bias, segment_extended, raw_chan.shape[1])


def scan_part(x_conv, b_conv, c_conv, dt_pre, bias_dt, log_rate, skip_gain, segment_extended):
    step_size = jax.nn.softplus(dt_pre + bias_dt[:, None])
    log_decay = step_size * (-jnp.exp(log_rate))[:, None]
    return span_terms(
        x_conv,
        b_conv,
        c_conv,
        step_size,
        log_decay,
        segment_extended[TAPS - 1 :],
        segment_extended[TAPS - 2],
        skip_gain,
    )


def weighted_sum(weight, stacked):
    return jnp.sum(weight[..., None, None] * stacked, axis=-3)


def span_fold(carry, states, state_start):
    blocks = carry.shape[-1]
    idx = jnp.arange(blocks)
    inside = (idx[None, :, None] < idx[None, None, :]) & (idx[None, None, :] < idx[:, None, None])
    link = jnp.prod(jnp.where(inside[None], carry[:, None, None, :], 1.0), axis=-1)
    link = link * (idx[None, :] < idx[:, None]).astype(jnp.float32)[None]
    lead = jnp.prod(jnp.where((idx[None, :] < idx[:, None])[None], carry[:, None, :], 1.0), axis=-1)
    tail = jnp.prod(jnp.where((idx[None, :] > idx[:, None])[None], carry[:, None, :], 1.0), axis=-1)
    starts = weighted_sum(link, states[:, None]) + lead[..., None, None] * state_start[:, None]
    state_end = weighted_sum(tail, states) + jnp.prod(carry, axis=-1)[:, None, None] * state_start
    return (jnp.moveaxis(starts, 1, 0), state_end)


def assemble(y_intra, c_three, entry, carry, states, state_start):
    starts, state_end = span_fold(carry, states, state_start)
    y_full = y_intra + jnp.einsum("nci,hci,chpn->hpci", c_three, entry, starts, precision=precise)
    return (y_full.reshape(y_full.shape[0] * y_full.shape[1], -1), state_end)


def reach(carry):

    def reach_advance(product, factor):
        return (product * factor, product)

    total, before = lax.scan(
        reach_advance, jnp.ones(carry.shape[:-1], jnp.float32), jnp.moveaxis(carry, -1, 0)
    )
    return (jnp.moveaxis(before, 0, -1), total)


def shards(
    x_in, b_in, c_in, dt_raw, cotangent, conv_weight, conv_bias, dt_bias, a_log, d_skip, doc_lengths
):
    lane = lax.axis_index("seq")
    x_width = x_in.shape[1]
    n_heads = dt_raw.shape[1]
    length = x_in.shape[2]
    blocks = length // SPAN
    groups_held = conv_weight.shape[0]
    packed = jnp.concatenate(
        [
            conv_weight.reshape(groups_held, -1),
            conv_bias,
            dt_bias,
            a_log,
            d_skip,
        ],
        axis=1,
    )
    count, here = (lax.axis_size("head"), lax.axis_index("head"))
    stacked = jnp.stack(
        [packed]
        + [
            lax.ppermute(packed, "head", [(i, (i + k) % count) for i in range(count)])
            for k in range(1, count)
        ]
    )
    order = (here - jnp.arange(count)) % count
    packed_all = jnp.take(stacked, order, axis=0).reshape((-1, packed.shape[1]))
    cuts = [conv_weight[0].size, conv_bias.shape[1], dt_bias.shape[1], a_log.shape[1]]
    bounds = [sum(cuts[:k]) for k in range(len(cuts) + 1)]
    weight_all = packed_all[:, : bounds[1]].reshape((-1,) + conv_weight.shape[1:])
    bias_all = packed_all[:, bounds[1] : bounds[2]]
    dt_bias_all = packed_all[:, bounds[2] : bounds[3]]
    a_log_all = packed_all[:, bounds[3] : bounds[4]]
    d_skip_all = packed_all[:, bounds[4] :]
    x_total = weight_all.shape[2] - 2 * STATE

    b_width = b_in.shape[1]

    def own_channels(table):
        pieces = [
            lax.dynamic_slice_in_dim(table, start + lane * width, width, axis=table.ndim - 1)
            for start, width in ((0, x_width), (x_total, b_width), (x_total + STATE, b_width))
        ]
        return (pieces[0], jnp.concatenate(pieces[1:], axis=table.ndim - 1))

    weight_x, weight_bc = own_channels(weight_all)
    bias_x, bias_bc = own_channels(bias_all)
    dt_bias_here = lax.dynamic_slice_in_dim(dt_bias_all, lane * n_heads, n_heads, axis=1)
    a_log_here = lax.dynamic_slice_in_dim(a_log_all, lane * n_heads, n_heads, axis=1)
    d_skip_here = lax.dynamic_slice_in_dim(d_skip_all, lane * n_heads, n_heads, axis=1)
    groups_here = x_in.shape[0]
    raw_chan = jnp.concatenate([x_in, b_in, c_in], axis=1)
    rim_chan = passed_along(raw_chan[:, :, length - (TAPS - 1) :], "head", 1)
    rank = lax.axis_index("head")
    positions = rank * length + jnp.arange(-(TAPS - 1), length, dtype=jnp.int32)
    segment_extended = segment_ids(positions, doc_lengths)
    each_group = (0, 0, 0, 0, None)

    def own_conv(x_float, bc_float, rim_float):
        x_conv = jax.vmap(conv_part, in_axes=each_group)(
            x_float, rim_float[:, :x_width], weight_x, bias_x, segment_extended
        )
        bc_conv = jax.vmap(conv_part, in_axes=each_group)(
            bc_float, rim_float[:, x_width:], weight_bc, bias_bc, segment_extended
        )
        return (x_conv, bc_conv)

    (x_conv, bc_conv), pull_conv = jax.vjp(
        own_conv,
        x_in.astype(jnp.float32),
        jnp.concatenate([b_in, c_in], axis=1).astype(jnp.float32),
        rim_chan.astype(jnp.float32),
    )
    both_conv = lax.all_gather(
        bc_conv.reshape(groups_here, 2, b_width, length), "seq", axis=2, tiled=True
    )
    b_conv, c_conv = (both_conv[:, 0], both_conv[:, 1])

    def local_terms(x_float, b_float, c_float, dt_float):
        return jax.vmap(scan_part, in_axes=(0, 0, 0, 0, 0, 0, 0, None))(
            x_float,
            b_float,
            c_float,
            dt_float,
            dt_bias_here,
            a_log_here,
            d_skip_here,
            segment_extended,
        )

    terms, pull_terms = jax.vjp(local_terms, x_conv, b_conv, c_conv, dt_raw.astype(jnp.float32))
    y_intra, c_three, entry, carry, states = terms
    before, total = reach(carry)
    state_zero = jnp.zeros((groups_here, n_heads, HEAD_DIM, STATE), jnp.float32)
    _, summary = jax.vmap(span_fold)(carry, states, state_zero)
    cot_float = cotangent.astype(jnp.float32)
    cot_five = cot_float.reshape(groups_here, n_heads, HEAD_DIM, blocks, SPAN)
    local_grad = jnp.einsum(
        "ghpci,ghci,gnci->ghpn", cot_five, entry * before[..., None], c_three, precision=precise
    )
    state_in, grad_out = carried_both(total, summary, local_grad, "head")

    def finish(pieces, state_start):
        return jax.vmap(assemble)(
            pieces[0], pieces[1], pieces[2], pieces[3], pieces[4], state_start
        )

    (y_scan, state_out), pull_out = jax.vjp(finish, terms, state_in)
    y_out = y_scan.astype(jnp.bfloat16)
    d_terms, _ = pull_out((cot_float, grad_out))
    d_x_conv, d_b_conv, d_c_conv, d_dt = pull_terms(d_terms)
    d_bc_conv = jnp.concatenate(
        [
            lax.psum_scatter(d_b_conv, "seq", scatter_dimension=1, tiled=True),
            lax.psum_scatter(d_c_conv, "seq", scatter_dimension=1, tiled=True),
        ],
        axis=1,
    )
    d_x, d_bc, d_rim = pull_conv((d_x_conv, d_bc_conv))
    d_raw = jnp.concatenate([d_x, d_bc], axis=1)
    returned = passed_along(d_rim, "head", -1)
    cut_at = length - (TAPS - 1)
    d_raw = jnp.concatenate([d_raw[:, :, :cut_at], d_raw[:, :, cut_at:] + returned], axis=2)
    x_grad = d_raw[:, :x_width].astype(jnp.bfloat16)
    b_grad = d_raw[:, x_width : x_width + b_width].astype(jnp.bfloat16)
    c_grad = d_raw[:, x_width + b_width :].astype(jnp.bfloat16)
    dt_grad = d_dt.astype(jnp.bfloat16)
    return (y_out, x_grad, b_grad, c_grad, dt_grad)


def solution(mesh):
    return jax.shard_map(
        shards,
        mesh=mesh,
        in_specs=(
            P(None, "seq", "head"),
            P(None, "seq", "head"),
            P(None, "seq", "head"),
            P(None, "seq", "head"),
            P(None, "seq", "head"),
            P("head", None, None),
            P("head", None),
            P("head", None),
            P("head", None),
            P("head", None),
            P(),
        ),
        out_specs=(
            P(None, "seq", "head"),
            P(None, "seq", "head"),
            P(None, "seq", "head"),
            P(None, "seq", "head"),
            P(None, "seq", "head"),
        ),
        check_vma=False,
    )
```

```python
import jax
import jax.numpy as jnp
from jax import lax
from jax.sharding import PartitionSpec as P

HEAD_DIM = 64
STATE = 256
TAPS = 4
SPAN = 128


precise = lax.Precision.HIGHEST


def passed_along(value, axis, steps):
    count = lax.axis_size(axis)
    first, last = (max(0, -steps), min(count, count - steps))
    return lax.ppermute(value, axis, [(source, source + steps) for source in range(first, last)])


def carried_both(totals, ahead, behind, axis):
    factor = totals[..., None, None]
    pair = lax.optimization_barrier((ahead, behind))
    received = lax.optimization_barrier(
        (passed_along(pair[0], axis, 1), passed_along(pair[1], axis, -1))
    )
    for _ in range(lax.axis_size(axis) - 2):
        received = lax.optimization_barrier(
            (
                passed_along(factor * received[0] + ahead, axis, 1),
                passed_along(factor * received[1] + behind, axis, -1),
            )
        )
    return received


def segment_ids(positions, doc_lengths):
    ends = jnp.cumsum(doc_lengths)
    counted = jnp.sum((ends[None, :] <= positions[:, None]).astype(jnp.int32), axis=1)
    return jnp.where(positions >= 0, counted, -1)


def conv_silu(padded, weight, bias, segment_extended, length):
    total = jnp.zeros((padded.shape[0], length), jnp.float32) + bias[:, None]
    for offset in range(TAPS):
        same_doc = (
            segment_extended[offset : offset + length] == segment_extended[TAPS - 1 :]
        ).astype(jnp.float32)
        total = (
            total
            + weight[offset][:, None] * padded[:, offset : offset + length] * same_doc[None, :]
        )
    return jax.nn.silu(total)


def span_terms(x_conv, b_conv, c_conv, step_size, log_decay, seg_tok, seg_before, skip_gain):
    n_heads, length = step_size.shape
    blocks = length // SPAN
    x_four = x_conv.reshape(n_heads, HEAD_DIM, blocks, SPAN)
    b_three = b_conv.reshape(STATE, blocks, SPAN)
    c_three = c_conv.reshape(STATE, blocks, SPAN)
    step_three = step_size.reshape(n_heads, blocks, SPAN)
    seg_two = seg_tok.reshape(blocks, SPAN)
    rows_idx = lax.broadcasted_iota(jnp.int32, (SPAN, SPAN), 0)
    cols_idx = lax.broadcasted_iota(jnp.int32, (SPAN, SPAN), 1)
    lower = (rows_idx >= cols_idx).astype(jnp.float32)
    cumul = jnp.einsum(
        "hcj,ij->hci", log_decay.reshape(n_heads, blocks, SPAN), lower, precision=precise
    )
    mask_doc = lower[None] * (seg_two[:, :, None] == seg_two[:, None, :]).astype(jnp.float32)
    decay = jnp.exp(jnp.minimum(cumul[:, :, :, None] - cumul[:, :, None, :], 0.0)) * mask_doc[None]
    scores = jnp.einsum("nci,ncj->cij", c_three, b_three, precision=precise)
    weighted = x_four * step_three[:, None]
    y_intra = jnp.einsum("hcij,hpcj->hpci", decay * scores[None], weighted, precision=precise)
    y_intra = y_intra + skip_gain[:, None, None, None] * x_four
    last_cum = cumul[:, :, -1:]
    keep_end = jnp.exp(last_cum - cumul) * (seg_two == seg_two[:, -1:]).astype(jnp.float32)[None]
    states = jnp.einsum("hpcj,hcj,ncj->hcpn", weighted, keep_end, b_three, precision=precise)
    prev_seg = jnp.concatenate([seg_before[None], seg_two[:-1, -1]])
    entry = jnp.exp(cumul) * (seg_two == prev_seg[:, None]).astype(jnp.float32)[None]
    carry = jnp.exp(last_cum[:, :, 0]) * (seg_two[:, -1] == prev_seg).astype(jnp.float32)[None]
    return (y_intra, c_three, entry, carry, states)


def group_terms(
    raw_chan, rim_chan, dt_pre, weight, bias, bias_dt, log_rate, skip_gain, segment_extended
):
    n_heads = dt_pre.shape[0]
    length = raw_chan.shape[1]
    padded = jnp.concatenate([rim_chan, raw_chan], axis=1)
    active = conv_silu(padded, weight, bias, segment_extended, length)
    split_at = n_heads * HEAD_DIM
    x_conv = active[:split_at]
    b_conv = active[split_at : split_at + STATE]
    c_conv = active[split_at + STATE :]
    step_size = jax.nn.softplus(dt_pre + bias_dt[:, None])
    log_decay = step_size * (-jnp.exp(log_rate))[:, None]
    return span_terms(
        x_conv,
        b_conv,
        c_conv,
        step_size,
        log_decay,
        segment_extended[TAPS - 1 :],
        segment_extended[TAPS - 2],
        skip_gain,
    )


def conv_part(raw_chan, rim_chan, weight, bias, segment_extended):
    padded = jnp.concatenate([rim_chan, raw_chan], axis=1)
    return conv_silu(padded, weight, bias, segment_extended, raw_chan.shape[1])


def scan_part(x_conv, b_conv, c_conv, dt_pre, bias_dt, log_rate, skip_gain, segment_extended):
    step_size = jax.nn.softplus(dt_pre + bias_dt[:, None])
    log_decay = step_size * (-jnp.exp(log_rate))[:, None]
    return span_terms(
        x_conv,
        b_conv,
        c_conv,
        step_size,
        log_decay,
        segment_extended[TAPS - 1 :],
        segment_extended[TAPS - 2],
        skip_gain,
    )


def weighted_sum(weight, stacked):
    return jnp.sum(weight[..., None, None] * stacked, axis=-3)


def span_fold(carry, states, state_start):
    blocks = carry.shape[-1]
    idx = jnp.arange(blocks)
    inside = (idx[None, :, None] < idx[None, None, :]) & (idx[None, None, :] < idx[:, None, None])
    link = jnp.prod(jnp.where(inside[None], carry[:, None, None, :], 1.0), axis=-1)
    link = link * (idx[None, :] < idx[:, None]).astype(jnp.float32)[None]
    lead = jnp.prod(jnp.where((idx[None, :] < idx[:, None])[None], carry[:, None, :], 1.0), axis=-1)
    tail = jnp.prod(jnp.where((idx[None, :] > idx[:, None])[None], carry[:, None, :], 1.0), axis=-1)
    starts = weighted_sum(link, states[:, None]) + lead[..., None, None] * state_start[:, None]
    state_end = weighted_sum(tail, states) + jnp.prod(carry, axis=-1)[:, None, None] * state_start
    return (jnp.moveaxis(starts, 1, 0), state_end)


def assemble(y_intra, c_three, entry, carry, states, state_start):
    starts, state_end = span_fold(carry, states, state_start)
    y_full = y_intra + jnp.einsum("nci,hci,chpn->hpci", c_three, entry, starts, precision=precise)
    return (y_full.reshape(y_full.shape[0] * y_full.shape[1], -1), state_end)


def reach(carry):

    def reach_advance(product, factor):
        return (product * factor, product)

    total, before = lax.scan(
        reach_advance, jnp.ones(carry.shape[:-1], jnp.float32), jnp.moveaxis(carry, -1, 0)
    )
    return (jnp.moveaxis(before, 0, -1), total)


def shards(
    x_in, b_in, c_in, dt_raw, cotangent, conv_weight, conv_bias, dt_bias, a_log, d_skip, doc_lengths
):
    lane = lax.axis_index("seq")
    x_width = x_in.shape[1]
    n_heads = dt_raw.shape[1]
    length = x_in.shape[2]
    blocks = length // SPAN
    groups_held = conv_weight.shape[0]
    packed = jnp.concatenate(
        [
            conv_weight.reshape(groups_held, -1),
            conv_bias,
            dt_bias,
            a_log,
            d_skip,
        ],
        axis=1,
    )
    count, here = (lax.axis_size("head"), lax.axis_index("head"))
    stacked = jnp.stack(
        [packed]
        + [
            lax.ppermute(packed, "head", [(i, (i + k) % count) for i in range(count)])
            for k in range(1, count)
        ]
    )
    order = (here - jnp.arange(count)) % count
    packed_all = jnp.take(stacked, order, axis=0).reshape((-1, packed.shape[1]))
    cuts = [conv_weight[0].size, conv_bias.shape[1], dt_bias.shape[1], a_log.shape[1]]
    bounds = [sum(cuts[:k]) for k in range(len(cuts) + 1)]
    weight_all = packed_all[:, : bounds[1]].reshape((-1,) + conv_weight.shape[1:])
    bias_all = packed_all[:, bounds[1] : bounds[2]]
    dt_bias_all = packed_all[:, bounds[2] : bounds[3]]
    a_log_all = packed_all[:, bounds[3] : bounds[4]]
    d_skip_all = packed_all[:, bounds[4] :]
    x_total = weight_all.shape[2] - 2 * STATE

    b_width = b_in.shape[1]

    def own_channels(table):
        pieces = [
            lax.dynamic_slice_in_dim(table, start + lane * width, width, axis=table.ndim - 1)
            for start, width in ((0, x_width), (x_total, b_width), (x_total + STATE, b_width))
        ]
        return (pieces[0], jnp.concatenate(pieces[1:], axis=table.ndim - 1))

    weight_x, weight_bc = own_channels(weight_all)
    bias_x, bias_bc = own_channels(bias_all)
    dt_bias_here = lax.dynamic_slice_in_dim(dt_bias_all, lane * n_heads, n_heads, axis=1)
    a_log_here = lax.dynamic_slice_in_dim(a_log_all, lane * n_heads, n_heads, axis=1)
    d_skip_here = lax.dynamic_slice_in_dim(d_skip_all, lane * n_heads, n_heads, axis=1)
    groups_here = x_in.shape[0]
    raw_chan = jnp.concatenate([x_in, b_in, c_in], axis=1)
    rim_chan = passed_along(raw_chan[:, :, length - (TAPS - 1) :], "head", 1)
    rank = lax.axis_index("head")
    positions = rank * length + jnp.arange(-(TAPS - 1), length, dtype=jnp.int32)
    segment_extended = segment_ids(positions, doc_lengths)
    each_group = (0, 0, 0, 0, None)

    def own_conv(x_float, bc_float, rim_float):
        x_conv = jax.vmap(conv_part, in_axes=each_group)(
            x_float, rim_float[:, :x_width], weight_x, bias_x, segment_extended
        )
        bc_conv = jax.vmap(conv_part, in_axes=each_group)(
            bc_float, rim_float[:, x_width:], weight_bc, bias_bc, segment_extended
        )
        return (x_conv, bc_conv)

    (x_conv, bc_conv), pull_conv = jax.vjp(
        own_conv,
        x_in.astype(jnp.float32),
        jnp.concatenate([b_in, c_in], axis=1).astype(jnp.float32),
        rim_chan.astype(jnp.float32),
    )
    lanes = lax.axis_size("seq")
    spread = jnp.stack(
        [bc_conv]
        + [
            lax.ppermute(bc_conv, "seq", [(i, (i + k) % lanes) for i in range(lanes)])
            for k in range(1, lanes)
        ]
    )
    spread = jnp.take(spread, (lane - jnp.arange(lanes)) % lanes, axis=0)
    b_conv = jnp.moveaxis(spread[:, :, :b_width], 0, 1).reshape(groups_here, -1, length)
    c_conv = jnp.moveaxis(spread[:, :, b_width:], 0, 1).reshape(groups_here, -1, length)

    def local_terms(x_float, b_float, c_float, dt_float):
        return jax.vmap(scan_part, in_axes=(0, 0, 0, 0, 0, 0, 0, None))(
            x_float,
            b_float,
            c_float,
            dt_float,
            dt_bias_here,
            a_log_here,
            d_skip_here,
            segment_extended,
        )

    terms, pull_terms = jax.vjp(local_terms, x_conv, b_conv, c_conv, dt_raw.astype(jnp.float32))
    y_intra, c_three, entry, carry, states = terms
    before, total = reach(carry)
    state_zero = jnp.zeros((groups_here, n_heads, HEAD_DIM, STATE), jnp.float32)
    _, summary = jax.vmap(span_fold)(carry, states, state_zero)
    cot_float = cotangent.astype(jnp.float32)
    cot_five = cot_float.reshape(groups_here, n_heads, HEAD_DIM, blocks, SPAN)
    local_grad = jnp.einsum(
        "ghpci,ghci,gnci->ghpn", cot_five, entry * before[..., None], c_three, precision=precise
    )
    state_in, grad_out = carried_both(total, summary, local_grad, "head")

    def finish(pieces, state_start):
        return jax.vmap(assemble)(
            pieces[0], pieces[1], pieces[2], pieces[3], pieces[4], state_start
        )

    (y_scan, state_out), pull_out = jax.vjp(finish, terms, state_in)
    y_out = y_scan.astype(jnp.bfloat16)
    d_terms, _ = pull_out((cot_float, grad_out))
    d_x_conv, d_b_conv, d_c_conv, d_dt = pull_terms(d_terms)
    d_bc_conv = jnp.concatenate(
        [
            lax.psum_scatter(d_b_conv, "seq", scatter_dimension=1, tiled=True),
            lax.psum_scatter(d_c_conv, "seq", scatter_dimension=1, tiled=True),
        ],
        axis=1,
    )
    d_x, d_bc, d_rim = pull_conv((d_x_conv, d_bc_conv))
    d_raw = jnp.concatenate([d_x, d_bc], axis=1)
    returned = passed_along(d_rim, "head", -1)
    cut_at = length - (TAPS - 1)
    d_raw = jnp.concatenate([d_raw[:, :, :cut_at], d_raw[:, :, cut_at:] + returned], axis=2)
    x_grad = d_raw[:, :x_width].astype(jnp.bfloat16)
    b_grad = d_raw[:, x_width : x_width + b_width].astype(jnp.bfloat16)
    c_grad = d_raw[:, x_width + b_width :].astype(jnp.bfloat16)
    dt_grad = d_dt.astype(jnp.bfloat16)
    return (y_out, x_grad, b_grad, c_grad, dt_grad)


def solution(mesh):
    return jax.shard_map(
        shards,
        mesh=mesh,
        in_specs=(
            P(None, "seq", "head"),
            P(None, "seq", "head"),
            P(None, "seq", "head"),
            P(None, "seq", "head"),
            P(None, "seq", "head"),
            P("head", None, None),
            P("head", None),
            P("head", None),
            P("head", None),
            P("head", None),
            P(),
        ),
        out_specs=(
            P(None, "seq", "head"),
            P(None, "seq", "head"),
            P(None, "seq", "head"),
            P(None, "seq", "head"),
            P(None, "seq", "head"),
        ),
        check_vma=False,
    )
```

```python
import jax
import jax.numpy as jnp
from jax import lax
from jax.sharding import PartitionSpec as P

HEAD_DIM = 64
STATE = 256
TAPS = 4
SPAN = 128


precise = lax.Precision.HIGHEST


def passed_along(value, axis, steps):
    count = lax.axis_size(axis)
    first, last = (max(0, -steps), min(count, count - steps))
    return lax.ppermute(value, axis, [(source, source + steps) for source in range(first, last)])


def carried_both(totals, ahead, behind, axis):
    factor = totals[..., None, None]
    pair = lax.optimization_barrier((ahead, behind))
    received = lax.optimization_barrier(
        (passed_along(pair[0], axis, 1), passed_along(pair[1], axis, -1))
    )
    for _ in range(lax.axis_size(axis) - 2):
        received = lax.optimization_barrier(
            (
                passed_along(factor * received[0] + ahead, axis, 1),
                passed_along(factor * received[1] + behind, axis, -1),
            )
        )
    return received


def segment_ids(positions, doc_lengths):
    ends = jnp.cumsum(doc_lengths)
    counted = jnp.sum((ends[None, :] <= positions[:, None]).astype(jnp.int32), axis=1)
    return jnp.where(positions >= 0, counted, -1)


def conv_silu(padded, weight, bias, segment_extended, length):
    total = jnp.zeros((padded.shape[0], length), jnp.float32) + bias[:, None]
    for offset in range(TAPS):
        same_doc = (
            segment_extended[offset : offset + length] == segment_extended[TAPS - 1 :]
        ).astype(jnp.float32)
        total = (
            total
            + weight[offset][:, None] * padded[:, offset : offset + length] * same_doc[None, :]
        )
    return jax.nn.silu(total)


def span_terms(x_conv, b_conv, c_conv, step_size, log_decay, seg_tok, seg_before, skip_gain):
    n_heads, length = step_size.shape
    blocks = length // SPAN
    x_four = x_conv.reshape(n_heads, HEAD_DIM, blocks, SPAN)
    b_three = b_conv.reshape(STATE, blocks, SPAN)
    c_three = c_conv.reshape(STATE, blocks, SPAN)
    step_three = step_size.reshape(n_heads, blocks, SPAN)
    seg_two = seg_tok.reshape(blocks, SPAN)
    rows_idx = lax.broadcasted_iota(jnp.int32, (SPAN, SPAN), 0)
    cols_idx = lax.broadcasted_iota(jnp.int32, (SPAN, SPAN), 1)
    lower = (rows_idx >= cols_idx).astype(jnp.float32)
    cumul = jnp.einsum(
        "hcj,ij->hci", log_decay.reshape(n_heads, blocks, SPAN), lower, precision=precise
    )
    mask_doc = lower[None] * (seg_two[:, :, None] == seg_two[:, None, :]).astype(jnp.float32)
    decay = jnp.exp(jnp.minimum(cumul[:, :, :, None] - cumul[:, :, None, :], 0.0)) * mask_doc[None]
    scores = jnp.einsum("nci,ncj->cij", c_three, b_three, precision=precise)
    weighted = x_four * step_three[:, None]
    y_intra = jnp.einsum("hcij,hpcj->hpci", decay * scores[None], weighted, precision=precise)
    y_intra = y_intra + skip_gain[:, None, None, None] * x_four
    last_cum = cumul[:, :, -1:]
    keep_end = jnp.exp(last_cum - cumul) * (seg_two == seg_two[:, -1:]).astype(jnp.float32)[None]
    states = jnp.einsum("hpcj,hcj,ncj->hcpn", weighted, keep_end, b_three, precision=precise)
    prev_seg = jnp.concatenate([seg_before[None], seg_two[:-1, -1]])
    entry = jnp.exp(cumul) * (seg_two == prev_seg[:, None]).astype(jnp.float32)[None]
    carry = jnp.exp(last_cum[:, :, 0]) * (seg_two[:, -1] == prev_seg).astype(jnp.float32)[None]
    return (y_intra, c_three, entry, carry, states)


def group_terms(
    raw_chan, rim_chan, dt_pre, weight, bias, bias_dt, log_rate, skip_gain, segment_extended
):
    n_heads = dt_pre.shape[0]
    length = raw_chan.shape[1]
    padded = jnp.concatenate([rim_chan, raw_chan], axis=1)
    active = conv_silu(padded, weight, bias, segment_extended, length)
    split_at = n_heads * HEAD_DIM
    x_conv = active[:split_at]
    b_conv = active[split_at : split_at + STATE]
    c_conv = active[split_at + STATE :]
    step_size = jax.nn.softplus(dt_pre + bias_dt[:, None])
    log_decay = step_size * (-jnp.exp(log_rate))[:, None]
    return span_terms(
        x_conv,
        b_conv,
        c_conv,
        step_size,
        log_decay,
        segment_extended[TAPS - 1 :],
        segment_extended[TAPS - 2],
        skip_gain,
    )


def conv_part(raw_chan, rim_chan, weight, bias, segment_extended):
    padded = jnp.concatenate([rim_chan, raw_chan], axis=1)
    return conv_silu(padded, weight, bias, segment_extended, raw_chan.shape[1])


def scan_part(x_conv, b_conv, c_conv, dt_pre, bias_dt, log_rate, skip_gain, segment_extended):
    step_size = jax.nn.softplus(dt_pre + bias_dt[:, None])
    log_decay = step_size * (-jnp.exp(log_rate))[:, None]
    return span_terms(
        x_conv,
        b_conv,
        c_conv,
        step_size,
        log_decay,
        segment_extended[TAPS - 1 :],
        segment_extended[TAPS - 2],
        skip_gain,
    )


def weighted_sum(weight, stacked):
    return jnp.sum(weight[..., None, None] * stacked, axis=-3)


def span_fold(carry, states, state_start):
    blocks = carry.shape[-1]
    idx = jnp.arange(blocks)
    inside = (idx[None, :, None] < idx[None, None, :]) & (idx[None, None, :] < idx[:, None, None])
    link = jnp.prod(jnp.where(inside[None], carry[:, None, None, :], 1.0), axis=-1)
    link = link * (idx[None, :] < idx[:, None]).astype(jnp.float32)[None]
    lead = jnp.prod(jnp.where((idx[None, :] < idx[:, None])[None], carry[:, None, :], 1.0), axis=-1)
    tail = jnp.prod(jnp.where((idx[None, :] > idx[:, None])[None], carry[:, None, :], 1.0), axis=-1)
    starts = weighted_sum(link, states[:, None]) + lead[..., None, None] * state_start[:, None]
    state_end = weighted_sum(tail, states) + jnp.prod(carry, axis=-1)[:, None, None] * state_start
    return (jnp.moveaxis(starts, 1, 0), state_end)


def assemble(y_intra, c_three, entry, carry, states, state_start):
    starts, state_end = span_fold(carry, states, state_start)
    y_full = y_intra + jnp.einsum("nci,hci,chpn->hpci", c_three, entry, starts, precision=precise)
    return (y_full.reshape(y_full.shape[0] * y_full.shape[1], -1), state_end)


def reach(carry):

    def reach_advance(product, factor):
        return (product * factor, product)

    total, before = lax.scan(
        reach_advance, jnp.ones(carry.shape[:-1], jnp.float32), jnp.moveaxis(carry, -1, 0)
    )
    return (jnp.moveaxis(before, 0, -1), total)


def shards(
    x_in, b_in, c_in, dt_raw, cotangent, conv_weight, conv_bias, dt_bias, a_log, d_skip, doc_lengths
):
    lane = lax.axis_index("seq")
    x_width = x_in.shape[1]
    n_heads = dt_raw.shape[1]
    length = x_in.shape[2]
    blocks = length // SPAN
    groups_held = conv_weight.shape[0]
    packed = jnp.concatenate(
        [
            conv_weight.reshape(groups_held, -1),
            conv_bias,
            dt_bias,
            a_log,
            d_skip,
        ],
        axis=1,
    )
    count, here = (lax.axis_size("head"), lax.axis_index("head"))
    stacked = jnp.stack(
        [packed]
        + [
            lax.ppermute(packed, "head", [(i, (i + k) % count) for i in range(count)])
            for k in range(1, count)
        ]
    )
    order = (here - jnp.arange(count)) % count
    packed_all = jnp.take(stacked, order, axis=0).reshape((-1, packed.shape[1]))
    cuts = [conv_weight[0].size, conv_bias.shape[1], dt_bias.shape[1], a_log.shape[1]]
    bounds = [sum(cuts[:k]) for k in range(len(cuts) + 1)]
    weight_all = packed_all[:, : bounds[1]].reshape((-1,) + conv_weight.shape[1:])
    bias_all = packed_all[:, bounds[1] : bounds[2]]
    dt_bias_all = packed_all[:, bounds[2] : bounds[3]]
    a_log_all = packed_all[:, bounds[3] : bounds[4]]
    d_skip_all = packed_all[:, bounds[4] :]
    x_total = weight_all.shape[2] - 2 * STATE

    b_width = b_in.shape[1]

    def own_channels(table):
        pieces = [
            lax.dynamic_slice_in_dim(table, start + lane * width, width, axis=table.ndim - 1)
            for start, width in ((0, x_width), (x_total, b_width), (x_total + STATE, b_width))
        ]
        return (pieces[0], jnp.concatenate(pieces[1:], axis=table.ndim - 1))

    weight_x, weight_bc = own_channels(weight_all)
    bias_x, bias_bc = own_channels(bias_all)
    dt_bias_here = lax.dynamic_slice_in_dim(dt_bias_all, lane * n_heads, n_heads, axis=1)
    a_log_here = lax.dynamic_slice_in_dim(a_log_all, lane * n_heads, n_heads, axis=1)
    d_skip_here = lax.dynamic_slice_in_dim(d_skip_all, lane * n_heads, n_heads, axis=1)
    groups_here = x_in.shape[0]
    raw_chan = jnp.concatenate([x_in, b_in, c_in], axis=1)
    rim_chan = passed_along(raw_chan[:, :, length - (TAPS - 1) :], "head", 1)
    rank = lax.axis_index("head")
    positions = rank * length + jnp.arange(-(TAPS - 1), length, dtype=jnp.int32)
    segment_extended = segment_ids(positions, doc_lengths)
    each_group = (0, 0, 0, 0, None)

    def own_conv(x_float, bc_float, rim_float):
        x_conv = jax.vmap(conv_part, in_axes=each_group)(
            x_float, rim_float[:, :x_width], weight_x, bias_x, segment_extended
        )
        bc_conv = jax.vmap(conv_part, in_axes=each_group)(
            bc_float, rim_float[:, x_width:], weight_bc, bias_bc, segment_extended
        )
        return (x_conv, bc_conv)

    (x_conv, bc_conv), pull_conv = jax.vjp(
        own_conv,
        x_in.astype(jnp.float32),
        jnp.concatenate([b_in, c_in], axis=1).astype(jnp.float32),
        rim_chan.astype(jnp.float32),
    )
    bc_every = jnp.concatenate(
        [
            lax.all_gather(b_in, "seq", axis=1, tiled=True),
            lax.all_gather(c_in, "seq", axis=1, tiled=True),
        ],
        axis=1,
    )
    rim_every = passed_along(bc_every[:, :, length - (TAPS - 1) :], "head", 1)
    every_conv = jax.vmap(conv_part, in_axes=each_group)(
        bc_every.astype(jnp.float32),
        rim_every.astype(jnp.float32),
        weight_all[:, :, x_total:],
        bias_all[:, x_total:],
        segment_extended,
    )
    b_conv, c_conv = (every_conv[:, :STATE], every_conv[:, STATE:])

    def local_terms(x_float, b_float, c_float, dt_float):
        return jax.vmap(scan_part, in_axes=(0, 0, 0, 0, 0, 0, 0, None))(
            x_float,
            b_float,
            c_float,
            dt_float,
            dt_bias_here,
            a_log_here,
            d_skip_here,
            segment_extended,
        )

    terms, pull_terms = jax.vjp(local_terms, x_conv, b_conv, c_conv, dt_raw.astype(jnp.float32))
    y_intra, c_three, entry, carry, states = terms
    before, total = reach(carry)
    state_zero = jnp.zeros((groups_here, n_heads, HEAD_DIM, STATE), jnp.float32)
    _, summary = jax.vmap(span_fold)(carry, states, state_zero)
    cot_float = cotangent.astype(jnp.float32)
    cot_five = cot_float.reshape(groups_here, n_heads, HEAD_DIM, blocks, SPAN)
    local_grad = jnp.einsum(
        "ghpci,ghci,gnci->ghpn", cot_five, entry * before[..., None], c_three, precision=precise
    )
    state_in, grad_out = carried_both(total, summary, local_grad, "head")

    def finish(pieces, state_start):
        return jax.vmap(assemble)(
            pieces[0], pieces[1], pieces[2], pieces[3], pieces[4], state_start
        )

    (y_scan, state_out), pull_out = jax.vjp(finish, terms, state_in)
    y_out = y_scan.astype(jnp.bfloat16)
    d_terms, _ = pull_out((cot_float, grad_out))
    d_x_conv, d_b_conv, d_c_conv, d_dt = pull_terms(d_terms)
    d_bc_conv = jnp.concatenate(
        [
            lax.psum_scatter(d_b_conv, "seq", scatter_dimension=1, tiled=True),
            lax.psum_scatter(d_c_conv, "seq", scatter_dimension=1, tiled=True),
        ],
        axis=1,
    )
    d_x, d_bc, d_rim = pull_conv((d_x_conv, d_bc_conv))
    d_raw = jnp.concatenate([d_x, d_bc], axis=1)
    returned = passed_along(d_rim, "head", -1)
    cut_at = length - (TAPS - 1)
    d_raw = jnp.concatenate([d_raw[:, :, :cut_at], d_raw[:, :, cut_at:] + returned], axis=2)
    x_grad = d_raw[:, :x_width].astype(jnp.bfloat16)
    b_grad = d_raw[:, x_width : x_width + b_width].astype(jnp.bfloat16)
    c_grad = d_raw[:, x_width + b_width :].astype(jnp.bfloat16)
    dt_grad = d_dt.astype(jnp.bfloat16)
    return (y_out, x_grad, b_grad, c_grad, dt_grad)


def solution(mesh):
    return jax.shard_map(
        shards,
        mesh=mesh,
        in_specs=(
            P(None, "seq", "head"),
            P(None, "seq", "head"),
            P(None, "seq", "head"),
            P(None, "seq", "head"),
            P(None, "seq", "head"),
            P("head", None, None),
            P("head", None),
            P("head", None),
            P("head", None),
            P("head", None),
            P(),
        ),
        out_specs=(
            P(None, "seq", "head"),
            P(None, "seq", "head"),
            P(None, "seq", "head"),
            P(None, "seq", "head"),
            P(None, "seq", "head"),
        ),
        check_vma=False,
    )
```
